32 devices in a mesh: parts: 2 (over y), blk: 4 (over z), grp: 2 (over x), fld: 2 (over core).
Axes of the slice: x: 2, y: 2, z: 4, core: 2. Of those that a mesh axis runs over, the one named last changes fastest.
Arguments:
- coords: float32 [32, 2, 2, 128], P(('parts', 'blk'), 'grp'), parts along dimension 0, may hold values from 0 to 1
- fields: float32 [32, 2, 64, 128], P(('parts', 'blk'), 'grp', 'fld'), parts along dimension 0, may hold values from -6 to 6
- neighbours: int32 [32, 2, 4], P(('parts', 'blk'), 'grp'), parts along dimension 0, may hold values from -1 to 29, as said below
Outputs:
- whitened: float32 [32, 2, 64, 128], P(('parts', 'blk'), 'grp', 'fld'), parts along dimension 0
- precision_product: float32 [32, 2, 64, 128], P(('parts', 'blk'), 'grp', 'fld'), parts along dimension 0
The draws below stay inside these ranges and needn't reach their ends.
There are 2 independent parts, one for each index of `parts`. The reference program is written for one: setup_inputs(seed, part) draws one part's arguments, and reference() takes and returns one part's arrays. A program takes and returns all parts, laid end to end along the dimension named above; each array names one. Nothing has to cross between parts.
Inputs may be any that keep to these rules, and one draw needn't show every extreme that they name: `neighbours`: each entry is -1 or the flat id j * 2 + h of a block with i - 8 <= j <= i - 1 and |h - g| <= 1, where (i, g) is the listing block; the ids of one list differ.
All inputs are finite; a program needn't handle non-finite values.
Results may differ from the reference program's by a relative error of at most 0.0003.
Values sent between devices are 32-bit elements; how exact they have to be, the bound alone decides.
No kernel may reach another device: no remote copies, remote signals or barrier semaphores. Data moves between devices by JAX's collectives and lax.ppermute only.
A program may use at most 64 MiB of HBM per device.

```python
import jax
import jax.numpy as jnp
from jax import lax

B = 128
CONDITION_SLOTS = 4
F = 64
WINDOW = 8
ORDER_PLACES = 16
SPATIAL_GROUPS = 2


def draw_neighbours(key, part):
    slot_codes = 3 * WINDOW
    first = jax.random.fold_in(key, 11)
    second_block = jax.random.fold_in(key, 23)
    distance_scores = jax.random.randint(first, (ORDER_PLACES, SPATIAL_GROUPS, slot_codes), 0, 2 ** 20) * slot_codes + jnp.arange(slot_codes, dtype=jnp.int32)
    order_pos = jnp.arange(ORDER_PLACES, dtype=jnp.int32)[:, None, None]
    group_pos = jnp.arange(SPATIAL_GROUPS, dtype=jnp.int32)[None, :, None]
    code_pos = jnp.arange(slot_codes, dtype=jnp.int32)[None, None, :]
    forced = (order_pos == ORDER_PLACES - 1) & (group_pos == SPATIAL_GROUPS - 1) & (code_pos == 1)
    distance_scores = distance_scores + jnp.where(forced, 2 ** 30, 0).astype(jnp.int32)
    chosen_blocks = lax.top_k(distance_scores, CONDITION_SLOTS)[0] % slot_codes
    back = chosen_blocks // 3 + 1
    side = chosen_blocks % 3 - 1
    earlier = order_pos - back
    group_of = group_pos + side
    neighbour_count = jax.random.randint(second_block, (ORDER_PLACES, SPATIAL_GROUPS, 1), 1, CONDITION_SLOTS + 1)
    slot_position = jnp.arange(CONDITION_SLOTS, dtype=jnp.int32)[None, None, :]
    valid = (earlier >= 0) & (group_of >= 0) & (group_of < SPATIAL_GROUPS) & (slot_position < neighbour_count)
    return jnp.where(valid, earlier * SPATIAL_GROUPS + group_of, -1).astype(jnp.int32)


def level_of(own_key, extent, shards, least, top_value):
    factor_of, own = 1.0, jax.random.fold_in(own_key, 6)
    for dim, blocks in shards:
        heights = jnp.exp(jax.random.uniform(jax.random.fold_in(own, dim), (blocks,), jnp.float32, least / len(shards), top_value / len(shards)))
        factor_of = factor_of * jnp.repeat(heights, extent[dim] // blocks).reshape([-1 if axis == dim else 1 for axis in range(len(extent))])
    return factor_of


def scatter_about(rng, dims, scale, reach, shards=(), kind=jnp.bfloat16):
    loudness = level_of(rng, dims, shards, -0.22, 0.18) if shards else 1.0
    drawn = jax.random.normal(rng, dims, jnp.float32) * scale * loudness
    return jnp.minimum(jnp.maximum(drawn, -reach), reach).astype(kind)


def setup_inputs(seed: int = 0, part: int = 0) -> dict:
    splits = jax.random.split(jax.random.key(seed), 4)
    part_keys = jax.random.split(jax.random.fold_in(splits[3], part), 4)
    return {
        "coords": jnp.clip(1.0 * jax.random.uniform(part_keys[0], (ORDER_PLACES, SPATIAL_GROUPS, 2, B), jnp.float32) ** level_of(part_keys[0], (ORDER_PLACES, SPATIAL_GROUPS, 2, B), ((0, 4), (1, 2)), -0.2, 0.2), 0.0, 1.0),
        "fields": scatter_about(part_keys[1], (ORDER_PLACES, SPATIAL_GROUPS, F, B), 1.0, 6.0, ((0, 4), (1, 2), (2, 2)), jnp.float32),
        "neighbours": draw_neighbours(jax.random.fold_in(jax.random.fold_in(splits[3], part), 71), part),
    }


ELL = 0.3
NUGGET = 0.25

def one_block(pts, vals, mask):
    count = pts.shape[0] * pts.shape[2]
    points = jnp.transpose(pts, (0, 2, 1)).reshape(count, 2)
    mpts = jnp.repeat(mask, pts.shape[2])
    delta_x = points[:, 0][:, None] - points[:, 0][None, :]
    delta_y = points[:, 1][:, None] - points[:, 1][None, :]
    scaled = jnp.sqrt(3.0) * jnp.sqrt(delta_x * delta_x + delta_y * delta_y) / ELL
    kernel = (1.0 + scaled) * jnp.exp(-scaled)
    cov = mpts[:, None] * mpts[None, :] * kernel + jnp.diag(NUGGET * mpts + 1.0 - mpts)
    factor = jnp.linalg.cholesky(cov)
    values = jnp.transpose(vals, (0, 2, 1)).reshape(count, vals.shape[1]) * mpts[:, None]
    solved = jax.scipy.linalg.solve_triangular(factor, values, lower=True)
    mine = solved[count - pts.shape[2]:]
    padded = jnp.concatenate([jnp.zeros((count - pts.shape[2], vals.shape[1]), jnp.float32), mine], axis=0)
    back = jax.scipy.linalg.solve_triangular(factor, padded, lower=True, trans='T') * mpts[:, None]
    back = jnp.transpose(back.reshape(pts.shape[0], pts.shape[2], vals.shape[1]), (0, 2, 1))
    return (mine.T, back)

def reference(coords, fields, neighbours):
    total_count = ORDER_PLACES * SPATIAL_GROUPS
    flat_coords = coords.reshape(total_count, 2, B)
    flat_fields = fields.reshape(total_count, F, B)
    neighbour_lists = neighbours.reshape(total_count, CONDITION_SLOTS)
    own_ids = jnp.arange(total_count, dtype=jnp.int32)
    slots = jnp.concatenate([neighbour_lists, own_ids[:, None]], axis=1)
    masks = (slots >= 0).astype(jnp.float32)
    safe = jnp.where(slots >= 0, slots, own_ids[:, None]).astype(jnp.int32)

    def visit(index, carry):
        whitened, product = carry
        rows = safe[index]
        white_block, back = one_block(flat_coords[rows], flat_fields[rows], masks[index])
        whitened = whitened.at[index].set(white_block)
        product = product.at[rows].add(back)
        return (whitened, product)
    start = (jnp.zeros((total_count, F, B), jnp.float32), jnp.zeros((total_count, F, B), jnp.float32))
    whitened, product = lax.fori_loop(0, total_count, visit, start)
    return (whitened.reshape(ORDER_PLACES, SPATIAL_GROUPS, F, B), product.reshape(ORDER_PLACES, SPATIAL_GROUPS, F, B))
```

```python
import jax
import jax.numpy as jnp
from jax import lax
from jax.sharding import PartitionSpec as P
from jax.experimental import pallas as pl

ELL = 0.3
NUGGET = 0.25


def padded_2(cells, sides, width):
    for axis, dim in sides:
        count = lax.axis_size(axis)
        ends = count - 1
        head = lax.slice_in_dim(cells, 0, width, axis=dim)
        tail = lax.slice_in_dim(cells, cells.shape[dim] - width, cells.shape[dim], axis=dim)
        cells = jnp.concatenate(
            [
                lax.ppermute(tail, axis, [(i, (i + 1) % count) for i in range(ends)]),
                cells,
                lax.ppermute(head, axis, [((i + 1) % count, i) for i in range(ends)]),
            ],
            axis=dim,
        )
    return cells


def shifted(block, axis, distance):
    devices = range(lax.axis_size(axis))
    route = [(i - distance, i) for i in devices if i - distance in devices]
    return lax.ppermute(block, axis, route)


def _diag_kernel(a_ref, u_ref, li_ref):
    g_count, n, _ = a_ref.shape
    rows = n // 8
    sub = lax.broadcasted_iota(jnp.int32, (8, n), 0)
    lane = lax.broadcasted_iota(jnp.int32, (8, n), 1)
    lefts, rights, scales = [], [], []
    for g in range(g_count):
        lefts.append([a_ref[g, 8 * r : 8 * r + 8, :] for r in range(rows)])
        rights.append(
            [jnp.where(lane == sub + 8 * r, 1.0, 0.0).astype(jnp.float32) for r in range(rows)]
        )
        scales.append([jnp.zeros((8, n), jnp.float32) for r in range(rows)])
    for j in range(n):
        r0, s = divmod(j, 8)
        for g in range(g_count):
            left, right, scale = lefts[g], rights[g], scales[g]
            row_l = jnp.broadcast_to(left[r0][s : s + 1, :], (8, n))
            row_r = jnp.broadcast_to(right[r0][s : s + 1, :], (8, n))
            piv = jnp.broadcast_to(row_l[:, j : j + 1], (8, n))
            inv = 1.0 / piv
            scale[r0] = jnp.where(sub == s, lax.rsqrt(piv), scale[r0])
            for r in range(r0, rows):
                f = jnp.broadcast_to(left[r][:, j : j + 1], (8, n)) * inv
                new_l = left[r] - f * row_l
                new_r = right[r] - f * row_r
                if r == r0:
                    new_l = jnp.where(sub > s, new_l, left[r])
                    new_r = jnp.where(sub > s, new_r, right[r])
                left[r] = new_l
                right[r] = new_r
    for g in range(g_count):
        for r in range(rows):
            upper = jnp.where(lane >= sub + 8 * r, lefts[g][r], 0.0)
            u_ref[g, 8 * r : 8 * r + 8, :] = upper * scales[g][r]
            li_ref[g, 8 * r : 8 * r + 8, :] = rights[g][r] * scales[g][r]


def diag_factor(a):
    shape = jax.ShapeDtypeStruct(a.shape, jnp.float32)
    return pl.pallas_call(_diag_kernel, out_shape=(shape, shape))(a)


def mm(spec, x, y):
    return jnp.einsum(spec, x, y, precision=lax.Precision.HIGHEST)


def many_blocks(pts, vals, mask):
    groups, slots, _, points = pts.shape
    count = slots * points
    fields = vals.shape[2]
    coords = jnp.transpose(pts, (0, 1, 3, 2)).reshape(groups, count, 2)
    mpts = jnp.repeat(mask, points, axis=1)
    delta_x = coords[:, :, 0][:, :, None] - coords[:, :, 0][:, None, :]
    delta_y = coords[:, :, 1][:, :, None] - coords[:, :, 1][:, None, :]
    scaled = jnp.sqrt(3.0) * jnp.sqrt(delta_x * delta_x + delta_y * delta_y) / ELL
    kernel = (1.0 + scaled) * jnp.exp(-scaled)
    eye = jnp.eye(count, dtype=jnp.float32)
    cov = mpts[:, :, None] * mpts[:, None, :] * kernel + eye * (NUGGET * mpts + 1.0 - mpts)[:, :, None]
    values = jnp.transpose(vals, (0, 1, 3, 2)).reshape(groups, count, fields) * mpts[:, :, None]
    trail = cov
    rest = values
    panels, inverses = [], []
    for k in range(slots):
        _, inv = diag_factor(trail[:, :points, :points])
        inverses.append(inv)
        white = mm("gij,gjf->gif", inv, rest[:, :points])
        if k < slots - 1:
            panel = mm("gic,gjc->gij", trail[:, points:, :points], inv)
            panels.append(panel)
            trail = trail[:, points:, points:] - mm("gic,gjc->gij", panel, panel)
            rest = rest[:, points:] - mm("gic,gcf->gif", panel, white)
    back = mm("gji,gjf->gif", inverses[-1], white)
    for k in range(slots - 2, -1, -1):
        rhs = -mm("gic,gif->gcf", panels[k], back)
        back = jnp.concatenate([mm("gji,gjf->gif", inverses[k], rhs), back], axis=1)
    back = back * mpts[:, :, None]
    back = jnp.transpose(back.reshape(groups, slots, points, fields), (0, 1, 3, 2))
    return jnp.transpose(white, (0, 2, 1)), back


def fetch_across(local):
    return padded_2(local, (("grp", 1),), 1)


def fetch_older(local):
    older = []
    for distance in (2, 1):
        older.append(shifted(local, "blk", distance))
    return jnp.concatenate(older + [local], axis=0)


def back_across(terms):
    total_count = terms[:, 1:2]
    for column, offset in ((0, -1), (2, 1)):
        total_count = total_count + shifted(terms[:, column : column + 1], "grp", offset)
    return total_count


def back_older(terms):
    per = terms.shape[0] // 3
    farthest = terms[:per]
    nearest = terms[per : 2 * per]
    total_count = terms[2 * per :]
    for distance, piece in ((1, nearest), (2, farthest)):
        total_count = total_count + shifted(piece, "blk", -distance)
    return total_count


def per_device(coords, fields, neighbours):
    per = coords.shape[0]
    local_fields = fields.shape[2]
    points = coords.shape[3]
    local = jnp.concatenate([coords, fields], axis=2)
    window = fetch_older(fetch_across(local))
    groups = lax.axis_size("grp")
    blk_pos = lax.axis_index("blk")
    grp_pos = lax.axis_index("grp")
    neighbour_lists = neighbours.reshape(per, neighbours.shape[2])
    earlier = neighbour_lists // groups - (blk_pos - 2) * per
    beside = neighbour_lists % groups - grp_pos + 1
    own_slot = ((2 * per + jnp.arange(per, dtype=jnp.int32)) * 3 + 1)[:, None]
    slots = jnp.concatenate(
        [jnp.where(neighbour_lists >= 0, earlier * 3 + beside, own_slot), own_slot], axis=1
    )
    masks = jnp.concatenate(
        [(neighbour_lists >= 0).astype(jnp.float32), jnp.ones((per, 1), jnp.float32)], axis=1
    )
    flat_window = window.reshape(9 * per, 2 + local_fields, points)
    width = slots.shape[1]
    all_fields = lax.all_gather(flat_window[:, 2:], "fld", axis=1, tiled=True)
    full_window = jnp.concatenate([flat_window[:, :2], all_fields], axis=1)
    half = per // lax.axis_size("fld")
    first = lax.axis_index("fld") * half
    my_slots = lax.dynamic_slice_in_dim(slots, first, half, 0)
    my_masks = lax.dynamic_slice_in_dim(masks, first, half, 0)

    rows = full_window[my_slots]
    mine_white, mine_backs = many_blocks(rows[:, :, :2], rows[:, :, 2:], my_masks)
    whitened, backs = (
        lax.all_to_all(mine_white[:, None], "fld", split_axis=2, concat_axis=0, tiled=True),
        lax.all_to_all(mine_backs, "fld", split_axis=2, concat_axis=0, tiled=True),
    )
    whitened = whitened[:, 0]
    onehot = (slots.reshape(-1)[None, :] == jnp.arange(9 * per, dtype=jnp.int32)[:, None]).astype(
        jnp.float32
    )
    onehot = onehot * masks.reshape(-1)[None, :]
    terms = jnp.dot(
        onehot, backs.reshape(width * per, local_fields * points), precision=lax.Precision.HIGHEST
    )
    terms = terms.reshape(3 * per, 3, local_fields, points)
    product = back_across(back_older(terms))
    return (whitened[:, None], product)


def solution(mesh):
    return jax.shard_map(
        per_device,
        mesh=mesh,
        in_specs=(
            P(("parts", "blk"), "grp", None, None),
            P(("parts", "blk"), "grp", "fld", None),
            P(("parts", "blk"), "grp", None),
        ),
        out_specs=(
            P(("parts", "blk"), "grp", "fld", None),
            P(("parts", "blk"), "grp", "fld", None),
        ),
        check_vma=False,
    )
```

```python
import jax
import jax.numpy as jnp
from jax import lax
from jax.sharding import PartitionSpec as P
from jax.experimental import pallas as pl

ELL = 0.3
NUGGET = 0.25


def padded_2(cells, sides, width):
    for axis, dim in sides:
        count = lax.axis_size(axis)
        ends = count - 1
        head = lax.slice_in_dim(cells, 0, width, axis=dim)
        tail = lax.slice_in_dim(cells, cells.shape[dim] - width, cells.shape[dim], axis=dim)
        cells = jnp.concatenate(
            [
                lax.ppermute(tail, axis, [(i, (i + 1) % count) for i in range(ends)]),
                cells,
                lax.ppermute(head, axis, [((i + 1) % count, i) for i in range(ends)]),
            ],
            axis=dim,
        )
    return cells


def shifted(block, axis, distance):
    devices = range(lax.axis_size(axis))
    route = [(i - distance, i) for i in devices if i - distance in devices]
    return lax.ppermute(block, axis, route)


def _diag_kernel(a_ref, u_ref, li_ref):
    g_count, n, _ = a_ref.shape
    rows = n // 8
    sub = lax.broadcasted_iota(jnp.int32, (8, n), 0)
    lane = lax.broadcasted_iota(jnp.int32, (8, n), 1)
    lefts, rights, scales = [], [], []
    for g in range(g_count):
        lefts.append([a_ref[g, 8 * r : 8 * r + 8, :] for r in range(rows)])
        rights.append(
            [jnp.where(lane == sub + 8 * r, 1.0, 0.0).astype(jnp.float32) for r in range(rows)]
        )
        scales.append([jnp.zeros((8, n), jnp.float32) for r in range(rows)])
    for j in range(n):
        r0, s = divmod(j, 8)
        for g in range(g_count):
            left, right, scale = lefts[g], rights[g], scales[g]
            row_l = jnp.broadcast_to(left[r0][s : s + 1, :], (8, n))
            row_r = jnp.broadcast_to(right[r0][s : s + 1, :], (8, n))
            piv = jnp.broadcast_to(row_l[:, j : j + 1], (8, n))
            inv = 1.0 / piv
            scale[r0] = jnp.where(sub == s, lax.rsqrt(piv), scale[r0])
            for r in range(r0, rows):
                f = jnp.broadcast_to(left[r][:, j : j + 1], (8, n)) * inv
                new_l = left[r] - f * row_l
                new_r = right[r] - f * row_r
                if r == r0:
                    new_l = jnp.where(sub > s, new_l, left[r])
                    new_r = jnp.where(sub > s, new_r, right[r])
                left[r] = new_l
                right[r] = new_r
    for g in range(g_count):
        for r in range(rows):
            upper = jnp.where(lane >= sub + 8 * r, lefts[g][r], 0.0)
            u_ref[g, 8 * r : 8 * r + 8, :] = upper * scales[g][r]
            li_ref[g, 8 * r : 8 * r + 8, :] = rights[g][r] * scales[g][r]


def diag_factor(a):
    shape = jax.ShapeDtypeStruct(a.shape, jnp.float32)
    return pl.pallas_call(_diag_kernel, out_shape=(shape, shape))(a)


def mm(spec, x, y):
    return jnp.einsum(spec, x, y, precision=lax.Precision.HIGHEST)


def many_blocks(pts, vals, mask):
    groups, slots, _, points = pts.shape
    count = slots * points
    fields = vals.shape[2]
    coords = jnp.transpose(pts, (0, 1, 3, 2)).reshape(groups, count, 2)
    mpts = jnp.repeat(mask, points, axis=1)
    delta_x = coords[:, :, 0][:, :, None] - coords[:, :, 0][:, None, :]
    delta_y = coords[:, :, 1][:, :, None] - coords[:, :, 1][:, None, :]
    scaled = jnp.sqrt(3.0) * jnp.sqrt(delta_x * delta_x + delta_y * delta_y) / ELL
    kernel = (1.0 + scaled) * jnp.exp(-scaled)
    eye = jnp.eye(count, dtype=jnp.float32)
    cov = mpts[:, :, None] * mpts[:, None, :] * kernel + eye * (NUGGET * mpts + 1.0 - mpts)[:, :, None]
    values = jnp.transpose(vals, (0, 1, 3, 2)).reshape(groups, count, fields) * mpts[:, :, None]
    trail = cov
    rest = values
    panels, inverses = [], []
    for k in range(slots):
        _, inv = diag_factor(trail[:, :points, :points])
        inverses.append(inv)
        white = mm("gij,gjf->gif", inv, rest[:, :points])
        if k < slots - 1:
            panel = mm("gic,gjc->gij", trail[:, points:, :points], inv)
            panels.append(panel)
            trail = trail[:, points:, points:] - mm("gic,gjc->gij", panel, panel)
            rest = rest[:, points:] - mm("gic,gcf->gif", panel, white)
    back = mm("gji,gjf->gif", inverses[-1], white)
    for k in range(slots - 2, -1, -1):
        rhs = -mm("gic,gif->gcf", panels[k], back)
        back = jnp.concatenate([mm("gji,gjf->gif", inverses[k], rhs), back], axis=1)
    back = back * mpts[:, :, None]
    back = jnp.transpose(back.reshape(groups, slots, points, fields), (0, 1, 3, 2))
    return jnp.transpose(white, (0, 2, 1)), back


def fetch_across(local):
    return padded_2(local, (("grp", 1),), 1)


def fetch_older(local):
    older = []
    for distance in (2, 1):
        older.append(shifted(local, "blk", distance))
    return jnp.concatenate(older + [local], axis=0)


def back_across(terms):
    total_count = terms[:, 1:2]
    for column, offset in ((0, -1), (2, 1)):
        total_count = total_count + shifted(terms[:, column : column + 1], "grp", offset)
    return total_count


def back_older(terms):
    per = terms.shape[0] // 3
    farthest = terms[:per]
    nearest = terms[per : 2 * per]
    total_count = terms[2 * per :]
    for distance, piece in ((1, nearest), (2, farthest)):
        total_count = total_count + shifted(piece, "blk", -distance)
    return total_count


def per_device(coords, fields, neighbours):
    per = coords.shape[0]
    window_coords = fetch_older(fetch_across(coords))
    window_fields = fetch_older(fetch_across(fields))
    groups = lax.axis_size("grp")
    blk_pos = lax.axis_index("blk")
    grp_pos = lax.axis_index("grp")
    neighbour_lists = neighbours.reshape(per, neighbours.shape[2])
    earlier = neighbour_lists // groups - (blk_pos - 2) * per
    beside = neighbour_lists % groups - grp_pos + 1
    own_slot = ((2 * per + jnp.arange(per, dtype=jnp.int32)) * 3 + 1)[:, None]
    slots = jnp.concatenate(
        [jnp.where(neighbour_lists >= 0, earlier * 3 + beside, own_slot), own_slot], axis=1
    )
    masks = jnp.concatenate(
        [(neighbour_lists >= 0).astype(jnp.float32), jnp.ones((per, 1), jnp.float32)], axis=1
    )
    flat_coords = window_coords.reshape((9 * per,) + coords.shape[2:])
    flat_fields = window_fields.reshape((9 * per,) + fields.shape[2:])
    width = slots.shape[1]
    local_fields = fields.shape[2]
    points = fields.shape[3]
    whitened, backs = many_blocks(flat_coords[slots], flat_fields[slots], masks)
    onehot = (slots.reshape(-1)[None, :] == jnp.arange(9 * per, dtype=jnp.int32)[:, None]).astype(
        jnp.float32
    )
    onehot = onehot * masks.reshape(-1)[None, :]
    terms = jnp.dot(
        onehot, backs.reshape(width * per, local_fields * points), precision=lax.Precision.HIGHEST
    )
    terms = terms.reshape(3 * per, 3, local_fields, points)
    product = back_across(back_older(terms))
    return (whitened[:, None], product)


def solution(mesh):
    return jax.shard_map(
        per_device,
        mesh=mesh,
        in_specs=(
            P(("parts", "blk"), "grp", None, None),
            P(("parts", "blk"), "grp", "fld", None),
            P(("parts", "blk"), "grp", None),
        ),
        out_specs=(
            P(("parts", "blk"), "grp", "fld", None),
            P(("parts", "blk"), "grp", "fld", None),
        ),
        check_vma=False,
    )
```

```python
import jax
import jax.numpy as jnp
from jax import lax
from jax.sharding import PartitionSpec as P
from jax.experimental import pallas as pl

ELL = 0.3
NUGGET = 0.25


def _diag_kernel(a_ref, u_ref, li_ref):
    g_count, n, _ = a_ref.shape
    rows = n // 8
    sub = lax.broadcasted_iota(jnp.int32, (8, n), 0)
    lane = lax.broadcasted_iota(jnp.int32, (8, n), 1)
    lefts, rights, scales = [], [], []
    for g in range(g_count):
        lefts.append([a_ref[g, 8 * r : 8 * r + 8, :] for r in range(rows)])
        rights.append(
            [jnp.where(lane == sub + 8 * r, 1.0, 0.0).astype(jnp.float32) for r in range(rows)]
        )
        scales.append([jnp.zeros((8, n), jnp.float32) for r in range(rows)])
    for j in range(n):
        r0, s = divmod(j, 8)
        for g in range(g_count):
            left, right, scale = lefts[g], rights[g], scales[g]
            row_l = jnp.broadcast_to(left[r0][s : s + 1, :], (8, n))
            row_r = jnp.broadcast_to(right[r0][s : s + 1, :], (8, n))
            piv = jnp.broadcast_to(row_l[:, j : j + 1], (8, n))
            inv = 1.0 / piv
            scale[r0] = jnp.where(sub == s, lax.rsqrt(piv), scale[r0])
            for r in range(r0, rows):
                f = jnp.broadcast_to(left[r][:, j : j + 1], (8, n)) * inv
                new_l = left[r] - f * row_l
                new_r = right[r] - f * row_r
                if r == r0:
                    new_l = jnp.where(sub > s, new_l, left[r])
                    new_r = jnp.where(sub > s, new_r, right[r])
                left[r] = new_l
                right[r] = new_r
    for g in range(g_count):
        for r in range(rows):
            upper = jnp.where(lane >= sub + 8 * r, lefts[g][r], 0.0)
            u_ref[g, 8 * r : 8 * r + 8, :] = upper * scales[g][r]
            li_ref[g, 8 * r : 8 * r + 8, :] = rights[g][r] * scales[g][r]


def diag_factor(a):
    shape = jax.ShapeDtypeStruct(a.shape, jnp.float32)
    return pl.pallas_call(_diag_kernel, out_shape=(shape, shape))(a)


def mm(spec, x, y):
    return jnp.einsum(spec, x, y, precision=lax.Precision.HIGHEST)


def many_blocks(pts, vals, mask):
    groups, slots, _, points = pts.shape
    count = slots * points
    fields = vals.shape[2]
    coords = jnp.transpose(pts, (0, 1, 3, 2)).reshape(groups, count, 2)
    mpts = jnp.repeat(mask, points, axis=1)
    delta_x = coords[:, :, 0][:, :, None] - coords[:, :, 0][:, None, :]
    delta_y = coords[:, :, 1][:, :, None] - coords[:, :, 1][:, None, :]
    scaled = jnp.sqrt(3.0) * jnp.sqrt(delta_x * delta_x + delta_y * delta_y) / ELL
    kernel = (1.0 + scaled) * jnp.exp(-scaled)
    eye = jnp.eye(count, dtype=jnp.float32)
    cov = mpts[:, :, None] * mpts[:, None, :] * kernel + eye * (NUGGET * mpts + 1.0 - mpts)[:, :, None]
    values = jnp.transpose(vals, (0, 1, 3, 2)).reshape(groups, count, fields) * mpts[:, :, None]
    trail = cov
    rest = values
    panels, inverses = [], []
    for k in range(slots):
        _, inv = diag_factor(trail[:, :points, :points])
        inverses.append(inv)
        white = mm("gij,gjf->gif", inv, rest[:, :points])
        if k < slots - 1:
            panel = mm("gic,gjc->gij", trail[:, points:, :points], inv)
            panels.append(panel)
            trail = trail[:, points:, points:] - mm("gic,gjc->gij", panel, panel)
            rest = rest[:, points:] - mm("gic,gcf->gif", panel, white)
    back = mm("gji,gjf->gif", inverses[-1], white)
    for k in range(slots - 2, -1, -1):
        rhs = -mm("gic,gif->gcf", panels[k], back)
        back = jnp.concatenate([mm("gji,gjf->gif", inverses[k], rhs), back], axis=1)
    back = back * mpts[:, :, None]
    back = jnp.transpose(back.reshape(groups, slots, points, fields), (0, 1, 3, 2))
    return jnp.transpose(white, (0, 2, 1)), back


def moved(block, blk_shift, grp_shift):
    blks = lax.axis_size("blk")
    grps = lax.axis_size("grp")
    route = []
    for b in range(blks):
        for g in range(grps):
            tb, tg = b + blk_shift, g + grp_shift
            if 0 <= tb < blks and 0 <= tg < grps:
                route.append((b * grps + g, tb * grps + tg))
    return lax.ppermute(block, ("blk", "grp"), route)


def fetch_window(local):
    rows = []
    for back in (2, 1, 0):
        row = []
        for side in (-1, 0, 1):
            row.append(local if back == 0 and side == 0 else moved(local, back, -side))
        rows.append(jnp.concatenate(row, axis=1))
    return jnp.concatenate(rows, axis=0)


def return_window(terms):
    per = terms.shape[0] // 3
    total = terms[2 * per :, 1]
    for index, back in enumerate((2, 1, 0)):
        for column, side in enumerate((-1, 0, 1)):
            if back == 0 and side == 0:
                continue
            piece = terms[index * per : (index + 1) * per, column]
            total = total + moved(piece, -back, side)
    return total[:, None]


def per_device(coords, fields, neighbours):
    per = coords.shape[0]
    window_coords = fetch_window(coords)
    window_fields = fetch_window(fields)
    groups = lax.axis_size("grp")
    blk_pos = lax.axis_index("blk")
    grp_pos = lax.axis_index("grp")
    neighbour_lists = neighbours.reshape(per, neighbours.shape[2])
    earlier = neighbour_lists // groups - (blk_pos - 2) * per
    beside = neighbour_lists % groups - grp_pos + 1
    own_slot = ((2 * per + jnp.arange(per, dtype=jnp.int32)) * 3 + 1)[:, None]
    slots = jnp.concatenate(
        [jnp.where(neighbour_lists >= 0, earlier * 3 + beside, own_slot), own_slot], axis=1
    )
    masks = jnp.concatenate(
        [(neighbour_lists >= 0).astype(jnp.float32), jnp.ones((per, 1), jnp.float32)], axis=1
    )
    flat_coords = window_coords.reshape((9 * per,) + coords.shape[2:])
    flat_fields = window_fields.reshape((9 * per,) + fields.shape[2:])
    width = slots.shape[1]
    local_fields = fields.shape[2]
    points = fields.shape[3]
    whitened, backs = many_blocks(flat_coords[slots], flat_fields[slots], masks)
    onehot = (slots.reshape(-1)[None, :] == jnp.arange(9 * per, dtype=jnp.int32)[:, None]).astype(
        jnp.float32
    )
    onehot = onehot * masks.reshape(-1)[None, :]
    terms = jnp.dot(
        onehot, backs.reshape(width * per, local_fields * points), precision=lax.Precision.HIGHEST
    )
    terms = terms.reshape(3 * per, 3, local_fields, points)
    product = return_window(terms)
    return (whitened[:, None], product)


def solution(mesh):
    return jax.shard_map(
        per_device,
        mesh=mesh,
        in_specs=(
            P(("parts", "blk"), "grp", None, None),
            P(("parts", "blk"), "grp", "fld", None),
            P(("parts", "blk"), "grp", None),
        ),
        out_specs=(
            P(("parts", "blk"), "grp", "fld", None),
            P(("parts", "blk"), "grp", "fld", None),
        ),
        check_vma=False,
    )
```

```python
import jax
import jax.numpy as jnp
from jax import lax
from jax.sharding import PartitionSpec as P
from jax.experimental import pallas as pl

ELL = 0.3
NUGGET = 0.25


def _diag_kernel(a_ref, u_ref, li_ref):
    g_count, n, _ = a_ref.shape
    rows = n // 8
    sub = lax.broadcasted_iota(jnp.int32, (8, n), 0)
    lane = lax.broadcasted_iota(jnp.int32, (8, n), 1)
    lefts, rights, scales = [], [], []
    for g in range(g_count):
        lefts.append([a_ref[g, 8 * r : 8 * r + 8, :] for r in range(rows)])
        rights.append(
            [jnp.where(lane == sub + 8 * r, 1.0, 0.0).astype(jnp.float32) for r in range(rows)]
        )
        scales.append([jnp.zeros((8, n), jnp.float32) for r in range(rows)])
    for j in range(n):
        r0, s = divmod(j, 8)
        for g in range(g_count):
            left, right, scale = lefts[g], rights[g], scales[g]
            row_l = jnp.broadcast_to(left[r0][s : s + 1, :], (8, n))
            row_r = jnp.broadcast_to(right[r0][s : s + 1, :], (8, n))
            piv = jnp.broadcast_to(row_l[:, j : j + 1], (8, n))
            inv = 1.0 / piv
            scale[r0] = jnp.where(sub == s, lax.rsqrt(piv), scale[r0])
            for r in range(r0, rows):
                f = jnp.broadcast_to(left[r][:, j : j + 1], (8, n)) * inv
                new_l = left[r] - f * row_l
                new_r = right[r] - f * row_r
                if r == r0:
                    new_l = jnp.where(sub > s, new_l, left[r])
                    new_r = jnp.where(sub > s, new_r, right[r])
                left[r] = new_l
                right[r] = new_r
    for g in range(g_count):
        for r in range(rows):
            upper = jnp.where(lane >= sub + 8 * r, lefts[g][r], 0.0)
            u_ref[g, 8 * r : 8 * r + 8, :] = upper * scales[g][r]
            li_ref[g, 8 * r : 8 * r + 8, :] = rights[g][r] * scales[g][r]


def diag_factor(a):
    shape = jax.ShapeDtypeStruct(a.shape, jnp.float32)
    return pl.pallas_call(_diag_kernel, out_shape=(shape, shape))(a)


def mm(spec, x, y):
    return jnp.einsum(spec, x, y, precision=lax.Precision.HIGHEST)


def many_blocks(pts, vals, mask):
    groups, slots, _, points = pts.shape
    count = slots * points
    fields = vals.shape[2]
    coords = jnp.transpose(pts, (0, 1, 3, 2)).reshape(groups, count, 2)
    mpts = jnp.repeat(mask, points, axis=1)
    delta_x = coords[:, :, 0][:, :, None] - coords[:, :, 0][:, None, :]
    delta_y = coords[:, :, 1][:, :, None] - coords[:, :, 1][:, None, :]
    scaled = jnp.sqrt(3.0) * jnp.sqrt(delta_x * delta_x + delta_y * delta_y) / ELL
    kernel = (1.0 + scaled) * jnp.exp(-scaled)
    eye = jnp.eye(count, dtype=jnp.float32)
    cov = mpts[:, :, None] * mpts[:, None, :] * kernel + eye * (NUGGET * mpts + 1.0 - mpts)[:, :, None]
    values = jnp.transpose(vals, (0, 1, 3, 2)).reshape(groups, count, fields) * mpts[:, :, None]
    trail = cov
    rest = values
    panels, inverses = [], []
    for k in range(slots):
        _, inv = diag_factor(trail[:, :points, :points])
        inverses.append(inv)
        white = mm("gij,gjf->gif", inv, rest[:, :points])
        if k < slots - 1:
            panel = mm("gic,gjc->gij", trail[:, points:, :points], inv)
            panels.append(panel)
            trail = trail[:, points:, points:] - mm("gic,gjc->gij", panel, panel)
            rest = rest[:, points:] - mm("gic,gcf->gif", panel, white)
    back = mm("gji,gjf->gif", inverses[-1], white)
    for k in range(slots - 2, -1, -1):
        rhs = -mm("gic,gif->gcf", panels[k], back)
        back = jnp.concatenate([mm("gji,gjf->gif", inverses[k], rhs), back], axis=1)
    back = back * mpts[:, :, None]
    back = jnp.transpose(back.reshape(groups, slots, points, fields), (0, 1, 3, 2))
    return jnp.transpose(white, (0, 2, 1)), back


def per_device(coords, fields, neighbours):
    per = coords.shape[0]
    groups = lax.axis_size("grp")
    blocks = lax.axis_size("blk") * groups * per
    blk_pos = lax.axis_index("blk")
    grp_pos = lax.axis_index("grp")
    all_coords = lax.all_gather(coords[:, 0], ("blk", "grp"), axis=0, tiled=False)
    all_fields = lax.all_gather(fields[:, 0], ("blk", "grp"), axis=0, tiled=False)
    all_coords = all_coords.reshape((blocks,) + coords.shape[2:])
    all_fields = all_fields.reshape((blocks,) + fields.shape[2:])
    neighbour_lists = neighbours.reshape(per, neighbours.shape[2])
    own_ids = (blk_pos * per + jnp.arange(per, dtype=jnp.int32)) * groups + grp_pos
    ids = jnp.concatenate(
        [jnp.where(neighbour_lists >= 0, neighbour_lists, own_ids[:, None]), own_ids[:, None]], axis=1
    )
    order = ids // groups
    slots = (order // per * groups + ids % groups) * per + order % per
    masks = jnp.concatenate(
        [(neighbour_lists >= 0).astype(jnp.float32), jnp.ones((per, 1), jnp.float32)], axis=1
    )
    width = slots.shape[1]
    local_fields = fields.shape[2]
    points = fields.shape[3]
    whitened, backs = many_blocks(all_coords[slots], all_fields[slots], masks)
    onehot = (slots.reshape(-1)[None, :] == jnp.arange(blocks, dtype=jnp.int32)[:, None]).astype(
        jnp.float32
    )
    onehot = onehot * masks.reshape(-1)[None, :]
    terms = jnp.dot(
        onehot, backs.reshape(width * per, local_fields * points), precision=lax.Precision.HIGHEST
    )
    terms = terms.reshape(blocks // per, per, local_fields, points)
    product = lax.psum_scatter(terms, ("blk", "grp"), scatter_dimension=0, tiled=False)
    return (whitened[:, None], product[:, None])


def solution(mesh):
    return jax.shard_map(
        per_device,
        mesh=mesh,
        in_specs=(
            P(("parts", "blk"), "grp", None, None),
            P(("parts", "blk"), "grp", "fld", None),
            P(("parts", "blk"), "grp", None),
        ),
        out_specs=(
            P(("parts", "blk"), "grp", "fld", None),
            P(("parts", "blk"), "grp", "fld", None),
        ),
        check_vma=False,
    )
```

```python
import jax
import jax.numpy as jnp
from jax import lax
from jax.sharding import PartitionSpec as P
from jax.experimental import pallas as pl
from jax.experimental.pallas import tpu as pltpu

ELL = 0.3
NUGGET = 0.25


def padded_2(cells, sides, width):
    for axis, dim in sides:
        count = lax.axis_size(axis)
        ends = count - 1
        head = lax.slice_in_dim(cells, 0, width, axis=dim)
        tail = lax.slice_in_dim(cells, cells.shape[dim] - width, cells.shape[dim], axis=dim)
        cells = jnp.concatenate(
            [
                lax.ppermute(tail, axis, [(i, (i + 1) % count) for i in range(ends)]),
                cells,
                lax.ppermute(head, axis, [((i + 1) % count, i) for i in range(ends)]),
            ],
            axis=dim,
        )
    return cells


def shifted(block, axis, distance):
    devices = range(lax.axis_size(axis))
    route = [(i - distance, i) for i in devices if i - distance in devices]
    return lax.ppermute(block, axis, route)


def _eliminate(a):
    n = a.shape[0]
    rows = n // 8
    sub = lax.broadcasted_iota(jnp.int32, (8, n), 0)
    lane = lax.broadcasted_iota(jnp.int32, (8, n), 1)
    left = [a[8 * r : 8 * r + 8, :] for r in range(rows)]
    right = [jnp.where(lane == sub + 8 * r, 1.0, 0.0).astype(jnp.float32) for r in range(rows)]
    scale = [jnp.zeros((8, n), jnp.float32) for r in range(rows)]
    return left, right, scale, sub


def _eliminate_all(mats):
    states = [_eliminate(a) for a in mats]
    n = mats[0].shape[0]
    rows = n // 8
    for j in range(n):
        r0, s = divmod(j, 8)
        for left, right, scale, sub in states:
            row_l = jnp.broadcast_to(left[r0][s : s + 1, :], (8, n))
            row_r = jnp.broadcast_to(right[r0][s : s + 1, :], (8, n))
            piv = jnp.broadcast_to(row_l[:, j : j + 1], (8, n))
            inv = 1.0 / piv
            scale[r0] = jnp.where(sub == s, lax.rsqrt(piv), scale[r0])
            for r in range(r0, rows):
                f = jnp.broadcast_to(left[r][:, j : j + 1], (8, n)) * inv
                new_l = left[r] - f * row_l
                new_r = right[r] - f * row_r
                if r == r0:
                    new_l = jnp.where(sub > s, new_l, left[r])
                    new_r = jnp.where(sub > s, new_r, right[r])
                left[r] = new_l
                right[r] = new_r
    return [
        jnp.concatenate([right[r] * scale[r] for r in range(rows)], axis=0)
        for left, right, scale, sub in states
    ]


def _dot(x, y, lhs_dim, rhs_dim):
    return lax.dot_general(
        x, y, (((lhs_dim,), (rhs_dim,)), ((), ())), precision=lax.Precision.HIGHEST,
        preferred_element_type=jnp.float32,
    )


def _fused_kernel(cov_ref, val_ref, white_ref, back_ref, trail, panels, inverses, rest):
    groups, slots, count, points = cov_ref.shape
    trail[...] = cov_ref[...]
    rest[...] = val_ref[...]
    row_id = lax.broadcasted_iota(jnp.int32, (count, points), 0)

    def forward(k, carry):
        start = pl.multiple_of(k * points, points)
        diag = [trail[g, k, pl.ds(start, points), :] for g in range(groups)]
        invs = _eliminate_all(diag)
        for g in range(groups):
            inv = invs[g]
            inverses[g, k] = inv
            panel = _dot(trail[g, k], inv, 1, 1)
            panel = jnp.where(row_id >= start + points, panel, 0.0)
            panels[g, k] = panel
            for c in range(slots):
                trail[g, c] = trail[g, c] - _dot(panel, panel[c * points : (c + 1) * points], 1, 1)
            white = _dot(inv, rest[g, pl.ds(start, points), :], 1, 0)
            rest[g] = rest[g] - _dot(panel, white, 1, 0)
            rest[g, pl.ds(start, points), :] = white
        return carry

    lax.fori_loop(0, slots, forward, 0)
    last = (slots - 1) * points
    for g in range(groups):
        white = rest[g, last:, :]
        white_ref[g] = white
        back_ref[g] = jnp.zeros(back_ref.shape[1:], jnp.float32)
        back_ref[g, last:, :] = _dot(inverses[g, slots - 1], white, 0, 0)

    def backward(step, carry):
        k = slots - 2 - step
        start = pl.multiple_of(k * points, points)
        for g in range(groups):
            rhs = _dot(panels[g, k], back_ref[g], 0, 0)
            back_ref[g, pl.ds(start, points), :] = -_dot(inverses[g, k], rhs, 0, 0)
        return carry

    lax.fori_loop(0, slots - 1, backward, 0)


def fused_solve(cov_blocks, values):
    groups, slots, count, points = cov_blocks.shape
    fields = values.shape[2]
    f32 = jnp.float32
    return pl.pallas_call(
        _fused_kernel,
        out_shape=(
            jax.ShapeDtypeStruct((groups, points, fields), f32),
            jax.ShapeDtypeStruct((groups, count, fields), f32),
        ),
        scratch_shapes=[
            pltpu.VMEM(cov_blocks.shape, f32),
            pltpu.VMEM(cov_blocks.shape, f32),
            pltpu.VMEM((groups, slots, points, points), f32),
            pltpu.VMEM(values.shape, f32),
        ],
        compiler_params=pltpu.CompilerParams(vmem_limit_bytes=100 * 1024 * 1024),
    )(cov_blocks, values)


def many_blocks(pts, vals, mask):
    groups, slots, _, points = pts.shape
    count = slots * points
    fields = vals.shape[2]
    coords = jnp.transpose(pts, (0, 1, 3, 2)).reshape(groups, count, 2)
    mpts = jnp.repeat(mask, points, axis=1)
    delta_x = coords[:, :, 0][:, :, None] - coords[:, :, 0][:, None, :]
    delta_y = coords[:, :, 1][:, :, None] - coords[:, :, 1][:, None, :]
    scaled = jnp.sqrt(3.0) * jnp.sqrt(delta_x * delta_x + delta_y * delta_y) / ELL
    kernel = (1.0 + scaled) * jnp.exp(-scaled)
    eye = jnp.eye(count, dtype=jnp.float32)
    cov = mpts[:, :, None] * mpts[:, None, :] * kernel + eye * (NUGGET * mpts + 1.0 - mpts)[:, :, None]
    cov_blocks = jnp.transpose(cov.reshape(groups, count, slots, points), (0, 2, 1, 3))
    values = jnp.transpose(vals, (0, 1, 3, 2)).reshape(groups, count, fields) * mpts[:, :, None]
    white, back = fused_solve(cov_blocks, values)
    back = back * mpts[:, :, None]
    back = jnp.transpose(back.reshape(groups, slots, points, fields), (0, 1, 3, 2))
    return jnp.transpose(white, (0, 2, 1)), back


def fetch_across(local):
    return padded_2(local, (("grp", 1),), 1)


def fetch_older(local):
    older = []
    for distance in (2, 1):
        older.append(shifted(local, "blk", distance))
    return jnp.concatenate(older + [local], axis=0)


def back_across(terms):
    total_count = terms[:, 1:2]
    for column, offset in ((0, -1), (2, 1)):
        total_count = total_count + shifted(terms[:, column : column + 1], "grp", offset)
    return total_count


def back_older(terms):
    per = terms.shape[0] // 3
    farthest = terms[:per]
    nearest = terms[per : 2 * per]
    total_count = terms[2 * per :]
    for distance, piece in ((1, nearest), (2, farthest)):
        total_count = total_count + shifted(piece, "blk", -distance)
    return total_count


def per_device(coords, fields, neighbours):
    per = coords.shape[0]
    window_coords = fetch_older(fetch_across(coords))
    window_fields = fetch_older(fetch_across(fields))
    groups = lax.axis_size("grp")
    blk_pos = lax.axis_index("blk")
    grp_pos = lax.axis_index("grp")
    neighbour_lists = neighbours.reshape(per, neighbours.shape[2])
    earlier = neighbour_lists // groups - (blk_pos - 2) * per
    beside = neighbour_lists % groups - grp_pos + 1
    own_slot = ((2 * per + jnp.arange(per, dtype=jnp.int32)) * 3 + 1)[:, None]
    slots = jnp.concatenate(
        [jnp.where(neighbour_lists >= 0, earlier * 3 + beside, own_slot), own_slot], axis=1
    )
    masks = jnp.concatenate(
        [(neighbour_lists >= 0).astype(jnp.float32), jnp.ones((per, 1), jnp.float32)], axis=1
    )
    flat_coords = window_coords.reshape((9 * per,) + coords.shape[2:])
    flat_fields = window_fields.reshape((9 * per,) + fields.shape[2:])
    width = slots.shape[1]
    local_fields = fields.shape[2]
    points = fields.shape[3]
    whitened, backs = many_blocks(flat_coords[slots], flat_fields[slots], masks)
    onehot = (slots.reshape(-1)[None, :] == jnp.arange(9 * per, dtype=jnp.int32)[:, None]).astype(
        jnp.float32
    )
    onehot = onehot * masks.reshape(-1)[None, :]
    terms = jnp.dot(
        onehot, backs.reshape(width * per, local_fields * points), precision=lax.Precision.HIGHEST
    )
    terms = terms.reshape(3 * per, 3, local_fields, points)
    product = back_across(back_older(terms))
    return (whitened[:, None], product)


def solution(mesh):
    return jax.shard_map(
        per_device,
        mesh=mesh,
        in_specs=(
            P(("parts", "blk"), "grp", None, None),
            P(("parts", "blk"), "grp", "fld", None),
            P(("parts", "blk"), "grp", None),
        ),
        out_specs=(
            P(("parts", "blk"), "grp", "fld", None),
            P(("parts", "blk"), "grp", "fld", None),
        ),
        check_vma=False,
    )
```

```python
import jax
import jax.numpy as jnp
from jax import lax
from jax.sharding import PartitionSpec as P
from jax.experimental import pallas as pl
from jax.experimental.pallas import tpu as pltpu

ELL = 0.3
NUGGET = 0.25


def padded_2(cells, sides, width):
    for axis, dim in sides:
        count = lax.axis_size(axis)
        ends = count - 1
        head = lax.slice_in_dim(cells, 0, width, axis=dim)
        tail = lax.slice_in_dim(cells, cells.shape[dim] - width, cells.shape[dim], axis=dim)
        cells = jnp.concatenate(
            [
                lax.ppermute(tail, axis, [(i, (i + 1) % count) for i in range(ends)]),
                cells,
                lax.ppermute(head, axis, [((i + 1) % count, i) for i in range(ends)]),
            ],
            axis=dim,
        )
    return cells


def shifted(block, axis, distance):
    devices = range(lax.axis_size(axis))
    route = [(i - distance, i) for i in devices if i - distance in devices]
    return lax.ppermute(block, axis, route)


def _eliminate(a):
    n = a.shape[0]
    rows = n // 8
    sub = lax.broadcasted_iota(jnp.int32, (8, n), 0)
    lane = lax.broadcasted_iota(jnp.int32, (8, n), 1)
    left = [a[8 * r : 8 * r + 8, :] for r in range(rows)]
    right = [jnp.where(lane == sub + 8 * r, 1.0, 0.0).astype(jnp.float32) for r in range(rows)]
    scale = [jnp.zeros((8, n), jnp.float32) for r in range(rows)]
    return left, right, scale, sub


def _eliminate_all(mats):
    states = [_eliminate(a) for a in mats]
    n = mats[0].shape[0]
    rows = n // 8
    for j in range(n):
        r0, s = divmod(j, 8)
        for left, right, scale, sub in states:
            row_l = jnp.broadcast_to(left[r0][s : s + 1, :], (8, n))
            row_r = jnp.broadcast_to(right[r0][s : s + 1, :], (8, n))
            piv = jnp.broadcast_to(row_l[:, j : j + 1], (8, n))
            inv = 1.0 / piv
            scale[r0] = jnp.where(sub == s, lax.rsqrt(piv), scale[r0])
            for r in range(r0, rows):
                f = jnp.broadcast_to(left[r][:, j : j + 1], (8, n)) * inv
                new_l = left[r] - f * row_l
                new_r = right[r] - f * row_r
                if r == r0:
                    new_l = jnp.where(sub > s, new_l, left[r])
                    new_r = jnp.where(sub > s, new_r, right[r])
                left[r] = new_l
                right[r] = new_r
    return [
        jnp.concatenate([right[r] * scale[r] for r in range(rows)], axis=0)
        for left, right, scale, sub in states
    ]


def _dot(x, y, lhs_dim, rhs_dim):
    return lax.dot_general(
        x, y, (((lhs_dim,), (rhs_dim,)), ((), ())), precision=lax.Precision.HIGHEST,
        preferred_element_type=jnp.float32,
    )


def _fused_kernel(cov_ref, val_ref, white_ref, back_ref, trail, panels, inverses, rest):
    groups, slots, count, points = cov_ref.shape
    trail[...] = cov_ref[...]
    rest[...] = val_ref[...]
    row_id = lax.broadcasted_iota(jnp.int32, (count, points), 0)

    def forward(k, carry):
        start = pl.multiple_of(k * points, points)
        diag = [trail[g, k, pl.ds(start, points), :] for g in range(groups)]
        invs = _eliminate_all(diag)
        for g in range(groups):
            inv = invs[g]
            inverses[g, k] = inv
            panel = _dot(trail[g, k], inv, 1, 1)
            panel = jnp.where(row_id >= start + points, panel, 0.0)
            panels[g, k] = panel

            def update(c, carry, g=g):
                lower = panels[g, k, pl.ds(pl.multiple_of(c * points, points), points), :]
                trail[g, c] = trail[g, c] - _dot(panels[g, k], lower, 1, 1)
                return carry

            lax.fori_loop(k + 1, slots, update, 0)
            white = _dot(inv, rest[g, pl.ds(start, points), :], 1, 0)
            rest[g] = rest[g] - _dot(panel, white, 1, 0)
            rest[g, pl.ds(start, points), :] = white
        return carry

    lax.fori_loop(0, slots, forward, 0)
    last = (slots - 1) * points
    for g in range(groups):
        white = rest[g, last:, :]
        white_ref[g] = white
        back_ref[g] = jnp.zeros(back_ref.shape[1:], jnp.float32)
        back_ref[g, last:, :] = _dot(inverses[g, slots - 1], white, 0, 0)

    def backward(step, carry):
        k = slots - 2 - step
        start = pl.multiple_of(k * points, points)
        for g in range(groups):
            rhs = _dot(panels[g, k], back_ref[g], 0, 0)
            back_ref[g, pl.ds(start, points), :] = -_dot(inverses[g, k], rhs, 0, 0)
        return carry

    lax.fori_loop(0, slots - 1, backward, 0)


def fused_solve(cov_blocks, values):
    groups, slots, count, points = cov_blocks.shape
    fields = values.shape[2]
    f32 = jnp.float32
    return pl.pallas_call(
        _fused_kernel,
        out_shape=(
            jax.ShapeDtypeStruct((groups, points, fields), f32),
            jax.ShapeDtypeStruct((groups, count, fields), f32),
        ),
        scratch_shapes=[
            pltpu.VMEM(cov_blocks.shape, f32),
            pltpu.VMEM(cov_blocks.shape, f32),
            pltpu.VMEM((groups, slots, points, points), f32),
            pltpu.VMEM(values.shape, f32),
        ],
        compiler_params=pltpu.CompilerParams(vmem_limit_bytes=100 * 1024 * 1024),
    )(cov_blocks, values)


def many_blocks(pts, vals, mask):
    groups, slots, _, points = pts.shape
    count = slots * points
    fields = vals.shape[2]
    coords = jnp.transpose(pts, (0, 1, 3, 2)).reshape(groups, count, 2)
    mpts = jnp.repeat(mask, points, axis=1)
    delta_x = coords[:, :, 0][:, :, None] - coords[:, :, 0][:, None, :]
    delta_y = coords[:, :, 1][:, :, None] - coords[:, :, 1][:, None, :]
    scaled = jnp.sqrt(3.0) * jnp.sqrt(delta_x * delta_x + delta_y * delta_y) / ELL
    kernel = (1.0 + scaled) * jnp.exp(-scaled)
    eye = jnp.eye(count, dtype=jnp.float32)
    cov = mpts[:, :, None] * mpts[:, None, :] * kernel + eye * (NUGGET * mpts + 1.0 - mpts)[:, :, None]
    cov_blocks = jnp.transpose(cov.reshape(groups, count, slots, points), (0, 2, 1, 3))
    values = jnp.transpose(vals, (0, 1, 3, 2)).reshape(groups, count, fields) * mpts[:, :, None]
    white, back = fused_solve(cov_blocks, values)
    back = back * mpts[:, :, None]
    back = jnp.transpose(back.reshape(groups, slots, points, fields), (0, 1, 3, 2))
    return jnp.transpose(white, (0, 2, 1)), back


def fetch_across(local):
    return padded_2(local, (("grp", 1),), 1)


def fetch_older(local):
    older = []
    for distance in (2, 1):
        older.append(shifted(local, "blk", distance))
    return jnp.concatenate(older + [local], axis=0)


def back_across(terms):
    total_count = terms[:, 1:2]
    for column, offset in ((0, -1), (2, 1)):
        total_count = total_count + shifted(terms[:, column : column + 1], "grp", offset)
    return total_count


def back_older(terms):
    per = terms.shape[0] // 3
    farthest = terms[:per]
    nearest = terms[per : 2 * per]
    total_count = terms[2 * per :]
    for distance, piece in ((1, nearest), (2, farthest)):
        total_count = total_count + shifted(piece, "blk", -distance)
    return total_count


def per_device(coords, fields, neighbours):
    per = coords.shape[0]
    window_coords = fetch_older(fetch_across(coords))
    window_fields = fetch_older(fetch_across(fields))
    groups = lax.axis_size("grp")
    blk_pos = lax.axis_index("blk")
    grp_pos = lax.axis_index("grp")
    neighbour_lists = neighbours.reshape(per, neighbours.shape[2])
    earlier = neighbour_lists // groups - (blk_pos - 2) * per
    beside = neighbour_lists % groups - grp_pos + 1
    own_slot = ((2 * per + jnp.arange(per, dtype=jnp.int32)) * 3 + 1)[:, None]
    slots = jnp.concatenate(
        [jnp.where(neighbour_lists >= 0, earlier * 3 + beside, own_slot), own_slot], axis=1
    )
    masks = jnp.concatenate(
        [(neighbour_lists >= 0).astype(jnp.float32), jnp.ones((per, 1), jnp.float32)], axis=1
    )
    flat_coords = window_coords.reshape((9 * per,) + coords.shape[2:])
    flat_fields = window_fields.reshape((9 * per,) + fields.shape[2:])
    width = slots.shape[1]
    local_fields = fields.shape[2]
    points = fields.shape[3]
    whitened, backs = many_blocks(flat_coords[slots], flat_fields[slots], masks)
    onehot = (slots.reshape(-1)[None, :] == jnp.arange(9 * per, dtype=jnp.int32)[:, None]).astype(
        jnp.float32
    )
    onehot = onehot * masks.reshape(-1)[None, :]
    terms = jnp.dot(
        onehot, backs.reshape(width * per, local_fields * points), precision=lax.Precision.HIGHEST
    )
    terms = terms.reshape(3 * per, 3, local_fields, points)
    product = back_across(back_older(terms))
    return (whitened[:, None], product)


def solution(mesh):
    return jax.shard_map(
        per_device,
        mesh=mesh,
        in_specs=(
            P(("parts", "blk"), "grp", None, None),
            P(("parts", "blk"), "grp", "fld", None),
            P(("parts", "blk"), "grp", None),
        ),
        out_specs=(
            P(("parts", "blk"), "grp", "fld", None),
            P(("parts", "blk"), "grp", "fld", None),
        ),
        check_vma=False,
    )
```

```python
import jax
import jax.numpy as jnp
from jax import lax
from jax.sharding import PartitionSpec as P
from jax.experimental import pallas as pl

ELL = 0.3
NUGGET = 0.25


def padded_2(cells, sides, width):
    for axis, dim in sides:
        count = lax.axis_size(axis)
        ends = count - 1
        head = lax.slice_in_dim(cells, 0, width, axis=dim)
        tail = lax.slice_in_dim(cells, cells.shape[dim] - width, cells.shape[dim], axis=dim)
        cells = jnp.concatenate(
            [
                lax.ppermute(tail, axis, [(i, (i + 1) % count) for i in range(ends)]),
                cells,
                lax.ppermute(head, axis, [((i + 1) % count, i) for i in range(ends)]),
            ],
            axis=dim,
        )
    return cells


def shifted(block, axis, distance):
    devices = range(lax.axis_size(axis))
    route = [(i - distance, i) for i in devices if i - distance in devices]
    return lax.ppermute(block, axis, route)


def _lane(x, j, n):
    return jnp.broadcast_to(x[:, j : j + 1], (8, n))


def _diag_kernel(a_ref, li_ref):
    g_count, n, _ = a_ref.shape
    rows = n // 8
    sub = lax.broadcasted_iota(jnp.int32, (8, n), 0)
    lane = lax.broadcasted_iota(jnp.int32, (8, n), 1)
    states = []
    for g in range(g_count):
        left = [a_ref[g, 8 * r : 8 * r + 8, :] for r in range(rows)]
        right = [jnp.where(lane == sub + 8 * r, 1.0, 0.0).astype(jnp.float32) for r in range(rows)]
        scale = [jnp.zeros((8, n), jnp.float32) for r in range(rows)]
        cols = {r: _lane(left[r], 0, n) for r in range(rows)}
        states.append((left, right, scale, cols))
    for j in range(n):
        r0, s = divmod(j, 8)
        for left, right, scale, cols in states:
            row_l = jnp.broadcast_to(left[r0][s : s + 1, :], (8, n))
            row_r = jnp.broadcast_to(right[r0][s : s + 1, :], (8, n))
            piv = jnp.broadcast_to(cols[r0][s : s + 1, :], (8, n))
            inv = 1.0 / piv
            scale[r0] = jnp.where(sub == s, lax.rsqrt(piv), scale[r0])
            if j + 1 < n:
                r1 = (j + 1) // 8
                ahead = {r: _lane(left[r], j + 1, n) for r in range(r1, rows)}
                cross = _lane(row_l, j + 1, n)
            for r in range(r0, rows):
                f = cols[r] * inv
                new_l = left[r] - f * row_l
                new_r = right[r] - f * row_r
                if r == r0:
                    new_l = jnp.where(sub > s, new_l, left[r])
                    new_r = jnp.where(sub > s, new_r, right[r])
                left[r] = new_l
                right[r] = new_r
                if j + 1 < n and r >= r1:
                    cols[r] = ahead[r] - f * cross
    for g in range(g_count):
        left, right, scale, cols = states[g]
        for r in range(rows):
            li_ref[g, 8 * r : 8 * r + 8, :] = right[r] * scale[r]


def diag_factor(a):
    return pl.pallas_call(_diag_kernel, out_shape=jax.ShapeDtypeStruct(a.shape, jnp.float32))(a)


def mm(spec, x, y):
    return jnp.einsum(spec, x, y, precision=lax.Precision.HIGHEST)


def many_blocks(pts, vals, mask):
    groups, slots, _, points = pts.shape
    count = slots * points
    fields = vals.shape[2]
    coords = jnp.transpose(pts, (0, 1, 3, 2)).reshape(groups, count, 2)
    mpts = jnp.repeat(mask, points, axis=1)
    delta_x = coords[:, :, 0][:, :, None] - coords[:, :, 0][:, None, :]
    delta_y = coords[:, :, 1][:, :, None] - coords[:, :, 1][:, None, :]
    scaled = jnp.sqrt(3.0) * jnp.sqrt(delta_x * delta_x + delta_y * delta_y) / ELL
    kernel = (1.0 + scaled) * jnp.exp(-scaled)
    eye = jnp.eye(count, dtype=jnp.float32)
    cov = mpts[:, :, None] * mpts[:, None, :] * kernel + eye * (NUGGET * mpts + 1.0 - mpts)[:, :, None]
    values = jnp.transpose(vals, (0, 1, 3, 2)).reshape(groups, count, fields) * mpts[:, :, None]
    trail = cov
    rest = values
    panels, inverses = [], []
    for k in range(slots):
        inv = diag_factor(trail[:, :points, :points])
        inverses.append(inv)
        white = mm("gij,gjf->gif", inv, rest[:, :points])
        if k < slots - 1:
            panel = mm("gic,gjc->gij", trail[:, points:, :points], inv)
            panels.append(panel)
            trail = trail[:, points:, points:] - mm("gic,gjc->gij", panel, panel)
            rest = rest[:, points:] - mm("gic,gcf->gif", panel, white)
    back = mm("gji,gjf->gif", inverses[-1], white)
    for k in range(slots - 2, -1, -1):
        rhs = -mm("gic,gif->gcf", panels[k], back)
        back = jnp.concatenate([mm("gji,gjf->gif", inverses[k], rhs), back], axis=1)
    back = back * mpts[:, :, None]
    back = jnp.transpose(back.reshape(groups, slots, points, fields), (0, 1, 3, 2))
    return jnp.transpose(white, (0, 2, 1)), back


def fetch_across(local):
    return padded_2(local, (("grp", 1),), 1)


def fetch_older(local):
    older = []
    for distance in (2, 1):
        older.append(shifted(local, "blk", distance))
    return jnp.concatenate(older + [local], axis=0)


def back_across(terms):
    total_count = terms[:, 1:2]
    for column, offset in ((0, -1), (2, 1)):
        total_count = total_count + shifted(terms[:, column : column + 1], "grp", offset)
    return total_count


def back_older(terms):
    per = terms.shape[0] // 3
    farthest = terms[:per]
    nearest = terms[per : 2 * per]
    total_count = terms[2 * per :]
    for distance, piece in ((1, nearest), (2, farthest)):
        total_count = total_count + shifted(piece, "blk", -distance)
    return total_count


def per_device(coords, fields, neighbours):
    per = coords.shape[0]
    window_coords = fetch_older(fetch_across(coords))
    window_fields = fetch_older(fetch_across(fields))
    groups = lax.axis_size("grp")
    blk_pos = lax.axis_index("blk")
    grp_pos = lax.axis_index("grp")
    neighbour_lists = neighbours.reshape(per, neighbours.shape[2])
    earlier = neighbour_lists // groups - (blk_pos - 2) * per
    beside = neighbour_lists % groups - grp_pos + 1
    own_slot = ((2 * per + jnp.arange(per, dtype=jnp.int32)) * 3 + 1)[:, None]
    slots = jnp.concatenate(
        [jnp.where(neighbour_lists >= 0, earlier * 3 + beside, own_slot), own_slot], axis=1
    )
    masks = jnp.concatenate(
        [(neighbour_lists >= 0).astype(jnp.float32), jnp.ones((per, 1), jnp.float32)], axis=1
    )
    flat_coords = window_coords.reshape((9 * per,) + coords.shape[2:])
    flat_fields = window_fields.reshape((9 * per,) + fields.shape[2:])
    width = slots.shape[1]
    local_fields = fields.shape[2]
    points = fields.shape[3]
    whitened, backs = many_blocks(flat_coords[slots], flat_fields[slots], masks)
    onehot = (slots.reshape(-1)[None, :] == jnp.arange(9 * per, dtype=jnp.int32)[:, None]).astype(
        jnp.float32
    )
    onehot = onehot * masks.reshape(-1)[None, :]
    terms = jnp.dot(
        onehot, backs.reshape(width * per, local_fields * points), precision=lax.Precision.HIGHEST
    )
    terms = terms.reshape(3 * per, 3, local_fields, points)
    product = back_across(back_older(terms))
    return (whitened[:, None], product)


def solution(mesh):
    return jax.shard_map(
        per_device,
        mesh=mesh,
        in_specs=(
            P(("parts", "blk"), "grp", None, None),
            P(("parts", "blk"), "grp", "fld", None),
            P(("parts", "blk"), "grp", None),
        ),
        out_specs=(
            P(("parts", "blk"), "grp", "fld", None),
            P(("parts", "blk"), "grp", "fld", None),
        ),
        check_vma=False,
    )
```

```python
import jax
import jax.numpy as jnp
from jax import lax
from jax.sharding import PartitionSpec as P
from jax.experimental import pallas as pl

ELL = 0.3
NUGGET = 0.25


def padded_2(cells, sides, width):
    for axis, dim in sides:
        count = lax.axis_size(axis)
        ends = count - 1
        head = lax.slice_in_dim(cells, 0, width, axis=dim)
        tail = lax.slice_in_dim(cells, cells.shape[dim] - width, cells.shape[dim], axis=dim)
        cells = jnp.concatenate(
            [
                lax.ppermute(tail, axis, [(i, (i + 1) % count) for i in range(ends)]),
                cells,
                lax.ppermute(head, axis, [((i + 1) % count, i) for i in range(ends)]),
            ],
            axis=dim,
        )
    return cells


def shifted(block, axis, distance):
    devices = range(lax.axis_size(axis))
    route = [(i - distance, i) for i in devices if i - distance in devices]
    return lax.ppermute(block, axis, route)


def _lane(x, j, n):
    return jnp.broadcast_to(x[:, j : j + 1], (8, n))


def _diag_kernel(a_ref, li_ref):
    g_count, n, _ = a_ref.shape
    rows = n // 8
    sub = lax.broadcasted_iota(jnp.int32, (8, n), 0)
    lane = lax.broadcasted_iota(jnp.int32, (8, n), 1)
    states = []
    for g in range(g_count):
        left = [a_ref[g, 8 * r : 8 * r + 8, :] for r in range(rows)]
        right = [jnp.where(lane == sub + 8 * r, 1.0, 0.0).astype(jnp.float32) for r in range(rows)]
        scale = [jnp.zeros((8, n), jnp.float32) for r in range(rows)]
        cols = {r: _lane(left[r], 0, n) for r in range(rows)}
        states.append((left, right, scale, cols))
    for j in range(n):
        r0, s = divmod(j, 8)
        for left, right, scale, cols in states:
            row_l = jnp.broadcast_to(left[r0][s : s + 1, :], (8, n))
            row_r = jnp.broadcast_to(right[r0][s : s + 1, :], (8, n))
            piv = jnp.broadcast_to(cols[r0][s : s + 1, :], (8, n))
            inv = 1.0 / piv
            scale[r0] = jnp.where(sub == s, lax.rsqrt(piv), scale[r0])
            if j + 1 < n:
                r1 = (j + 1) // 8
                ahead = {r: _lane(left[r], j + 1, n) for r in range(r1, rows)}
                cross = _lane(row_l, j + 1, n)
                cross = cross * inv
            row_l = row_l * inv
            row_r = row_r * inv
            for r in range(r0, rows):
                new_l = left[r] - cols[r] * row_l
                new_r = right[r] - cols[r] * row_r
                if r == r0:
                    new_l = jnp.where(sub > s, new_l, left[r])
                    new_r = jnp.where(sub > s, new_r, right[r])
                left[r] = new_l
                right[r] = new_r
                if j + 1 < n and r >= r1:
                    cols[r] = ahead[r] - cols[r] * cross
    for g in range(g_count):
        left, right, scale, cols = states[g]
        for r in range(rows):
            li_ref[g, 8 * r : 8 * r + 8, :] = right[r] * scale[r]


def diag_factor(a, points):
    groups, _, _ = a.shape
    block = (groups, points, points)
    return pl.pallas_call(
        _diag_kernel,
        out_shape=jax.ShapeDtypeStruct(block, jnp.float32),
        grid=(1,),
        in_specs=[pl.BlockSpec(block, lambda i: (0, 0, 0))],
        out_specs=pl.BlockSpec(block, lambda i: (0, 0, 0)),
    )(a)


def mm(spec, x, y):
    return jnp.einsum(spec, x, y, precision=lax.Precision.HIGHEST)


def many_blocks(pts, vals, mask):
    groups, slots, _, points = pts.shape
    count = slots * points
    fields = vals.shape[2]
    coords = jnp.transpose(pts, (0, 1, 3, 2)).reshape(groups, count, 2)
    mpts = jnp.repeat(mask, points, axis=1)
    delta_x = coords[:, :, 0][:, :, None] - coords[:, :, 0][:, None, :]
    delta_y = coords[:, :, 1][:, :, None] - coords[:, :, 1][:, None, :]
    scaled = jnp.sqrt(3.0) * jnp.sqrt(delta_x * delta_x + delta_y * delta_y) / ELL
    kernel = (1.0 + scaled) * jnp.exp(-scaled)
    eye = jnp.eye(count, dtype=jnp.float32)
    cov = mpts[:, :, None] * mpts[:, None, :] * kernel + eye * (NUGGET * mpts + 1.0 - mpts)[:, :, None]
    values = jnp.transpose(vals, (0, 1, 3, 2)).reshape(groups, count, fields) * mpts[:, :, None]
    trail = cov
    rest = values
    panels, inverses = [], []
    for k in range(slots):
        inv = diag_factor(trail, points)
        inverses.append(inv)
        white = mm("gij,gjf->gif", inv, rest[:, :points])
        if k < slots - 1:
            panel = mm("gic,gjc->gij", trail[:, points:, :points], inv)
            panels.append(panel)
            trail = trail[:, points:, points:] - mm("gic,gjc->gij", panel, panel)
            rest = rest[:, points:] - mm("gic,gcf->gif", panel, white)
    back = mm("gji,gjf->gif", inverses[-1], white)
    for k in range(slots - 2, -1, -1):
        rhs = -mm("gic,gif->gcf", panels[k], back)
        back = jnp.concatenate([mm("gji,gjf->gif", inverses[k], rhs), back], axis=1)
    back = back * mpts[:, :, None]
    back = jnp.transpose(back.reshape(groups, slots, points, fields), (0, 1, 3, 2))
    return jnp.transpose(white, (0, 2, 1)), back


def fetch_across(local):
    return padded_2(local, (("grp", 1),), 1)


def fetch_older(local):
    older = []
    for distance in (2, 1):
        older.append(shifted(local, "blk", distance))
    return jnp.concatenate(older + [local], axis=0)


def back_across(terms):
    total_count = terms[:, 1:2]
    for column, offset in ((0, -1), (2, 1)):
        total_count = total_count + shifted(terms[:, column : column + 1], "grp", offset)
    return total_count


def back_older(terms):
    per = terms.shape[0] // 3
    farthest = terms[:per]
    nearest = terms[per : 2 * per]
    total_count = terms[2 * per :]
    for distance, piece in ((1, nearest), (2, farthest)):
        total_count = total_count + shifted(piece, "blk", -distance)
    return total_count


def per_device(coords, fields, neighbours):
    per = coords.shape[0]
    window_coords = fetch_older(fetch_across(coords))
    window_fields = fetch_older(fetch_across(fields))
    groups = lax.axis_size("grp")
    blk_pos = lax.axis_index("blk")
    grp_pos = lax.axis_index("grp")
    neighbour_lists = neighbours.reshape(per, neighbours.shape[2])
    earlier = neighbour_lists // groups - (blk_pos - 2) * per
    beside = neighbour_lists % groups - grp_pos + 1
    own_slot = ((2 * per + jnp.arange(per, dtype=jnp.int32)) * 3 + 1)[:, None]
    slots = jnp.concatenate(
        [jnp.where(neighbour_lists >= 0, earlier * 3 + beside, own_slot), own_slot], axis=1
    )
    masks = jnp.concatenate(
        [(neighbour_lists >= 0).astype(jnp.float32), jnp.ones((per, 1), jnp.float32)], axis=1
    )
    flat_coords = window_coords.reshape((9 * per,) + coords.shape[2:])
    flat_fields = window_fields.reshape((9 * per,) + fields.shape[2:])
    width = slots.shape[1]
    local_fields = fields.shape[2]
    points = fields.shape[3]
    whitened, backs = many_blocks(flat_coords[slots], flat_fields[slots], masks)
    onehot = (slots.reshape(-1)[None, :] == jnp.arange(9 * per, dtype=jnp.int32)[:, None]).astype(
        jnp.float32
    )
    onehot = onehot * masks.reshape(-1)[None, :]
    terms = jnp.dot(
        onehot, backs.reshape(width * per, local_fields * points), precision=lax.Precision.HIGHEST
    )
    terms = terms.reshape(3 * per, 3, local_fields, points)
    product = back_across(back_older(terms))
    return (whitened[:, None], product)


def solution(mesh):
    return jax.shard_map(
        per_device,
        mesh=mesh,
        in_specs=(
            P(("parts", "blk"), "grp", None, None),
            P(("parts", "blk"), "grp", "fld", None),
            P(("parts", "blk"), "grp", None),
        ),
        out_specs=(
            P(("parts", "blk"), "grp", "fld", None),
            P(("parts", "blk"), "grp", "fld", None),
        ),
        check_vma=False,
    )
```

```python
import jax
import jax.numpy as jnp
from jax import lax
from jax.sharding import PartitionSpec as P
from jax.experimental import pallas as pl

ELL = 0.3
NUGGET = 0.25


def padded_2(cells, sides, width):
    for axis, dim in sides:
        count = lax.axis_size(axis)
        ends = count - 1
        head = lax.slice_in_dim(cells, 0, width, axis=dim)
        tail = lax.slice_in_dim(cells, cells.shape[dim] - width, cells.shape[dim], axis=dim)
        cells = jnp.concatenate(
            [
                lax.ppermute(tail, axis, [(i, (i + 1) % count) for i in range(ends)]),
                cells,
                lax.ppermute(head, axis, [((i + 1) % count, i) for i in range(ends)]),
            ],
            axis=dim,
        )
    return cells


def shifted(block, axis, distance):
    devices = range(lax.axis_size(axis))
    route = [(i - distance, i) for i in devices if i - distance in devices]
    return lax.ppermute(block, axis, route)


def _lane(x, j, n):
    return jnp.broadcast_to(x[:, j : j + 1], (8, n))


def _diag_kernel(a_ref, li_ref):
    g_count, n, _ = a_ref.shape
    rows = n // 8
    sub = lax.broadcasted_iota(jnp.int32, (8, n), 0)
    lane = lax.broadcasted_iota(jnp.int32, (8, n), 1)
    states = []
    for g in range(g_count):
        left = [a_ref[g, 8 * r : 8 * r + 8, :] for r in range(rows)]
        right = [jnp.where(lane == sub + 8 * r, 1.0, 0.0).astype(jnp.float32) for r in range(rows)]
        scale = [jnp.zeros((8, n), jnp.float32) for r in range(rows)]
        cols = {r: _lane(left[r], 0, n) for r in range(rows)}
        states.append((left, right, scale, cols))
    for j in range(n):
        r0, s = divmod(j, 8)
        for left, right, scale, cols in states:
            row_l = jnp.broadcast_to(left[r0][s : s + 1, :], (8, n))
            row_r = jnp.broadcast_to(right[r0][s : s + 1, :], (8, n))
            piv = jnp.broadcast_to(cols[r0][s : s + 1, :], (8, n))
            inv = 1.0 / piv
            scale[r0] = jnp.where(sub == s, lax.rsqrt(piv), scale[r0])
            if j + 1 < n:
                r1 = (j + 1) // 8
                ahead = {r: _lane(left[r], j + 1, n) for r in range(r1, rows)}
                cross = _lane(row_l, j + 1, n)
                cross = cross * inv
            row_l = row_l * inv
            row_r = row_r * inv
            for r in range(r0, rows):
                new_l = left[r] - cols[r] * row_l
                new_r = right[r] - cols[r] * row_r
                if r == r0:
                    new_l = jnp.where(sub > s, new_l, left[r])
                    new_r = jnp.where(sub > s, new_r, right[r])
                left[r] = new_l
                right[r] = new_r
                if j + 1 < n and r >= r1:
                    cols[r] = ahead[r] - cols[r] * cross
    for g in range(g_count):
        left, right, scale, cols = states[g]
        for r in range(rows):
            li_ref[g, 8 * r : 8 * r + 8, :] = right[r] * scale[r]


def diag_factor(a, points):
    groups, _, _ = a.shape
    block = (groups, points, points)
    return pl.pallas_call(
        _diag_kernel,
        out_shape=jax.ShapeDtypeStruct(block, jnp.float32),
        grid=(1,),
        in_specs=[pl.BlockSpec(block, lambda i: (0, 0, 0))],
        out_specs=pl.BlockSpec(block, lambda i: (0, 0, 0)),
    )(a)


def mm(spec, x, y):
    return jnp.einsum(spec, x, y, precision=lax.Precision.HIGHEST)


def many_blocks(pts, vals, mask):
    groups, slots, _, points = pts.shape
    count = slots * points
    fields = vals.shape[2]
    coords = jnp.transpose(pts, (0, 1, 3, 2)).reshape(groups, count, 2)
    mpts = jnp.repeat(mask, points, axis=1)
    delta_x = coords[:, :, 0][:, :, None] - coords[:, :, 0][:, None, :]
    delta_y = coords[:, :, 1][:, :, None] - coords[:, :, 1][:, None, :]
    scaled = jnp.sqrt(3.0) * jnp.sqrt(delta_x * delta_x + delta_y * delta_y) / ELL
    kernel = (1.0 + scaled) * jnp.exp(-scaled)
    eye = jnp.eye(count, dtype=jnp.float32)
    cov = mpts[:, :, None] * mpts[:, None, :] * kernel + eye * (NUGGET * mpts + 1.0 - mpts)[:, :, None]
    values = jnp.transpose(vals, (0, 1, 3, 2)).reshape(groups, count, fields) * mpts[:, :, None]
    lower = []
    panels, inverses, solved = [], [], []
    for k in range(slots):
        top = k * points
        column = cov[:, top:, top : top + points]
        rhs = values[:, top : top + points]
        if k:
            done = jnp.concatenate(lower, axis=2)
            column = column - mm("gic,gjc->gij", done[:, top:], done[:, top : top + points])
            rhs = rhs - mm("gic,gcf->gif", done[:, top : top + points], jnp.concatenate(solved, axis=1))
        inv = diag_factor(column, points)
        inverses.append(inv)
        white = mm("gij,gjf->gif", inv, rhs)
        solved.append(white)
        if k < slots - 1:
            panel = mm("gic,gjc->gij", column[:, points:], inv)
            panels.append(panel)
            lower.append(jnp.pad(panel, ((0, 0), (top + points, 0), (0, 0))))
    back = mm("gji,gjf->gif", inverses[-1], white)
    for k in range(slots - 2, -1, -1):
        rhs = -mm("gic,gif->gcf", panels[k], back)
        back = jnp.concatenate([mm("gji,gjf->gif", inverses[k], rhs), back], axis=1)
    back = back * mpts[:, :, None]
    back = jnp.transpose(back.reshape(groups, slots, points, fields), (0, 1, 3, 2))
    return jnp.transpose(white, (0, 2, 1)), back


def fetch_across(local):
    return padded_2(local, (("grp", 1),), 1)


def fetch_older(local):
    older = []
    for distance in (2, 1):
        older.append(shifted(local, "blk", distance))
    return jnp.concatenate(older + [local], axis=0)


def back_across(terms):
    total_count = terms[:, 1:2]
    for column, offset in ((0, -1), (2, 1)):
        total_count = total_count + shifted(terms[:, column : column + 1], "grp", offset)
    return total_count


def back_older(terms):
    per = terms.shape[0] // 3
    farthest = terms[:per]
    nearest = terms[per : 2 * per]
    total_count = terms[2 * per :]
    for distance, piece in ((1, nearest), (2, farthest)):
        total_count = total_count + shifted(piece, "blk", -distance)
    return total_count


def per_device(coords, fields, neighbours):
    per = coords.shape[0]
    window_coords = fetch_older(fetch_across(coords))
    window_fields = fetch_older(fetch_across(fields))
    groups = lax.axis_size("grp")
    blk_pos = lax.axis_index("blk")
    grp_pos = lax.axis_index("grp")
    neighbour_lists = neighbours.reshape(per, neighbours.shape[2])
    earlier = neighbour_lists // groups - (blk_pos - 2) * per
    beside = neighbour_lists % groups - grp_pos + 1
    own_slot = ((2 * per + jnp.arange(per, dtype=jnp.int32)) * 3 + 1)[:, None]
    slots = jnp.concatenate(
        [jnp.where(neighbour_lists >= 0, earlier * 3 + beside, own_slot), own_slot], axis=1
    )
    masks = jnp.concatenate(
        [(neighbour_lists >= 0).astype(jnp.float32), jnp.ones((per, 1), jnp.float32)], axis=1
    )
    flat_coords = window_coords.reshape((9 * per,) + coords.shape[2:])
    flat_fields = window_fields.reshape((9 * per,) + fields.shape[2:])
    width = slots.shape[1]
    local_fields = fields.shape[2]
    points = fields.shape[3]
    whitened, backs = many_blocks(flat_coords[slots], flat_fields[slots], masks)
    onehot = (slots.reshape(-1)[None, :] == jnp.arange(9 * per, dtype=jnp.int32)[:, None]).astype(
        jnp.float32
    )
    onehot = onehot * masks.reshape(-1)[None, :]
    terms = jnp.dot(
        onehot, backs.reshape(width * per, local_fields * points), precision=lax.Precision.HIGHEST
    )
    terms = terms.reshape(3 * per, 3, local_fields, points)
    product = back_across(back_older(terms))
    return (whitened[:, None], product)


def solution(mesh):
    return jax.shard_map(
        per_device,
        mesh=mesh,
        in_specs=(
            P(("parts", "blk"), "grp", None, None),
            P(("parts", "blk"), "grp", "fld", None),
            P(("parts", "blk"), "grp", None),
        ),
        out_specs=(
            P(("parts", "blk"), "grp", "fld", None),
            P(("parts", "blk"), "grp", "fld", None),
        ),
        check_vma=False,
    )
```

```python
import jax
import jax.numpy as jnp
from jax import lax
from jax.sharding import PartitionSpec as P
from jax.experimental import pallas as pl

ELL = 0.3
NUGGET = 0.25


def padded_2(cells, sides, width):
    for axis, dim in sides:
        count = lax.axis_size(axis)
        ends = count - 1
        head = lax.slice_in_dim(cells, 0, width, axis=dim)
        tail = lax.slice_in_dim(cells, cells.shape[dim] - width, cells.shape[dim], axis=dim)
        cells = jnp.concatenate(
            [
                lax.ppermute(tail, axis, [(i, (i + 1) % count) for i in range(ends)]),
                cells,
                lax.ppermute(head, axis, [((i + 1) % count, i) for i in range(ends)]),
            ],
            axis=dim,
        )
    return cells


def shifted(block, axis, distance):
    devices = range(lax.axis_size(axis))
    route = [(i - distance, i) for i in devices if i - distance in devices]
    return lax.ppermute(block, axis, route)


def _lane(x, j, n):
    return jnp.broadcast_to(x[:, j : j + 1], (8, n))


def _diag_kernel(a_ref, li_ref):
    g_count, n, _ = a_ref.shape
    rows = n // 8
    sub = lax.broadcasted_iota(jnp.int32, (8, n), 0)
    lane = lax.broadcasted_iota(jnp.int32, (8, n), 1)
    states = []
    for g in range(g_count):
        left = [a_ref[g, 8 * r : 8 * r + 8, :] for r in range(rows)]
        right = [jnp.where(lane == sub + 8 * r, 1.0, 0.0).astype(jnp.float32) for r in range(rows)]
        scale = [jnp.zeros((8, n), jnp.float32) for r in range(rows)]
        cols = {r: _lane(left[r], 0, n) for r in range(rows)}
        states.append((left, right, scale, cols))
    for j in range(n):
        r0, s = divmod(j, 8)
        for left, right, scale, cols in states:
            row_l = jnp.broadcast_to(left[r0][s : s + 1, :], (8, n))
            row_r = jnp.broadcast_to(right[r0][s : s + 1, :], (8, n))
            piv = jnp.broadcast_to(cols[r0][s : s + 1, :], (8, n))
            inv = 1.0 / piv
            scale[r0] = jnp.where(sub == s, lax.rsqrt(piv), scale[r0])
            if j + 1 < n:
                r1 = (j + 1) // 8
                ahead = {r: _lane(left[r], j + 1, n) for r in range(r1, rows)}
                cross = _lane(row_l, j + 1, n)
                cross = cross * inv
            row_l = row_l * inv
            row_r = row_r * inv
            for r in range(r0, rows):
                new_l = left[r] - cols[r] * row_l
                new_r = right[r] - cols[r] * row_r
                if r == r0:
                    new_l = jnp.where(sub > s, new_l, left[r])
                    new_r = jnp.where(sub > s, new_r, right[r])
                left[r] = new_l
                right[r] = new_r
                if j + 1 < n and r >= r1:
                    cols[r] = ahead[r] - cols[r] * cross
    for g in range(g_count):
        left, right, scale, cols = states[g]
        for r in range(rows):
            li_ref[g, 8 * r : 8 * r + 8, :] = right[r] * scale[r]


def diag_factor(a, points):
    groups, _, _ = a.shape
    block = (groups, points, points)
    return pl.pallas_call(
        _diag_kernel,
        out_shape=jax.ShapeDtypeStruct(block, jnp.float32),
        grid=(1,),
        in_specs=[pl.BlockSpec(block, lambda i: (0, 0, 0))],
        out_specs=pl.BlockSpec(block, lambda i: (0, 0, 0)),
    )(a)


def mm(spec, x, y):
    return jnp.einsum(spec, x, y, precision=lax.Precision.HIGHEST)


def many_blocks(pts, gather_vals, mask, late=2):
    groups, slots, _, points = pts.shape
    count = slots * points
    coords = jnp.transpose(pts, (0, 1, 3, 2)).reshape(groups, count, 2)
    mpts = jnp.repeat(mask, points, axis=1)
    delta_x = coords[:, :, 0][:, :, None] - coords[:, :, 0][:, None, :]
    delta_y = coords[:, :, 1][:, :, None] - coords[:, :, 1][:, None, :]
    scaled = jnp.sqrt(3.0) * jnp.sqrt(delta_x * delta_x + delta_y * delta_y) / ELL
    kernel = (1.0 + scaled) * jnp.exp(-scaled)
    eye = jnp.eye(count, dtype=jnp.float32)
    cov = mpts[:, :, None] * mpts[:, None, :] * kernel + eye * (NUGGET * mpts + 1.0 - mpts)[:, :, None]
    trail = cov
    panels, inverses = [], []
    rest = None
    solved = 0
    for k in range(slots):
        inv = diag_factor(trail, points)
        inverses.append(inv)
        if k == 0:
            vals = gather_vals(inv)
            fields = vals.shape[2]
            values = jnp.transpose(vals, (0, 1, 3, 2)).reshape(groups, count, fields)
            rest = values * mpts[:, :, None]
        if k < slots - 1:
            panel = mm("gic,gjc->gij", trail[:, points:, :points], inv)
            panels.append(panel)
            trail = trail[:, points:, points:] - mm("gic,gjc->gij", panel, panel)
        if k >= min(late, slots - 1):
            while solved <= k:
                white = mm("gij,gjf->gif", inverses[solved], rest[:, :points])
                if solved < slots - 1:
                    rest = rest[:, points:] - mm("gic,gcf->gif", panels[solved], white)
                solved += 1
    back = mm("gji,gjf->gif", inverses[-1], white)
    for k in range(slots - 2, -1, -1):
        rhs = -mm("gic,gif->gcf", panels[k], back)
        back = jnp.concatenate([mm("gji,gjf->gif", inverses[k], rhs), back], axis=1)
    back = back * mpts[:, :, None]
    back = jnp.transpose(back.reshape(groups, slots, points, fields), (0, 1, 3, 2))
    return jnp.transpose(white, (0, 2, 1)), back


def fetch_across(local):
    return padded_2(local, (("grp", 1),), 1)


def fetch_older(local):
    older = []
    for distance in (2, 1):
        older.append(shifted(local, "blk", distance))
    return jnp.concatenate(older + [local], axis=0)


def back_across(terms):
    total_count = terms[:, 1:2]
    for column, offset in ((0, -1), (2, 1)):
        total_count = total_count + shifted(terms[:, column : column + 1], "grp", offset)
    return total_count


def back_older(terms):
    per = terms.shape[0] // 3
    farthest = terms[:per]
    nearest = terms[per : 2 * per]
    total_count = terms[2 * per :]
    for distance, piece in ((1, nearest), (2, farthest)):
        total_count = total_count + shifted(piece, "blk", -distance)
    return total_count


def per_device(coords, fields, neighbours):
    per = coords.shape[0]
    window_coords = fetch_older(fetch_across(coords))
    groups = lax.axis_size("grp")
    blk_pos = lax.axis_index("blk")
    grp_pos = lax.axis_index("grp")
    neighbour_lists = neighbours.reshape(per, neighbours.shape[2])
    earlier = neighbour_lists // groups - (blk_pos - 2) * per
    beside = neighbour_lists % groups - grp_pos + 1
    own_slot = ((2 * per + jnp.arange(per, dtype=jnp.int32)) * 3 + 1)[:, None]
    slots = jnp.concatenate(
        [jnp.where(neighbour_lists >= 0, earlier * 3 + beside, own_slot), own_slot], axis=1
    )
    masks = jnp.concatenate(
        [(neighbour_lists >= 0).astype(jnp.float32), jnp.ones((per, 1), jnp.float32)], axis=1
    )
    flat_coords = window_coords.reshape((9 * per,) + coords.shape[2:])
    width = slots.shape[1]
    local_fields = fields.shape[2]
    points = fields.shape[3]

    def gather_vals(after):
        _, local = lax.optimization_barrier((after, fields))
        window_fields = fetch_older(fetch_across(local))
        flat_fields = window_fields.reshape((9 * per,) + fields.shape[2:])
        return flat_fields[slots]

    whitened, backs = many_blocks(flat_coords[slots], gather_vals, masks)
    onehot = (slots.reshape(-1)[None, :] == jnp.arange(9 * per, dtype=jnp.int32)[:, None]).astype(
        jnp.float32
    )
    onehot = onehot * masks.reshape(-1)[None, :]
    terms = jnp.dot(
        onehot, backs.reshape(width * per, local_fields * points), precision=lax.Precision.HIGHEST
    )
    terms = terms.reshape(3 * per, 3, local_fields, points)
    product = back_across(back_older(terms))
    return (whitened[:, None], product)


def solution(mesh):
    return jax.shard_map(
        per_device,
        mesh=mesh,
        in_specs=(
            P(("parts", "blk"), "grp", None, None),
            P(("parts", "blk"), "grp", "fld", None),
            P(("parts", "blk"), "grp", None),
        ),
        out_specs=(
            P(("parts", "blk"), "grp", "fld", None),
            P(("parts", "blk"), "grp", "fld", None),
        ),
        check_vma=False,
    )
```

```python
import jax
import jax.numpy as jnp
from jax import lax
from jax.sharding import PartitionSpec as P
from jax.experimental import pallas as pl

ELL = 0.3
NUGGET = 0.25


def padded_2(cells, sides, width):
    for axis, dim in sides:
        count = lax.axis_size(axis)
        ends = count - 1
        head = lax.slice_in_dim(cells, 0, width, axis=dim)
        tail = lax.slice_in_dim(cells, cells.shape[dim] - width, cells.shape[dim], axis=dim)
        cells = jnp.concatenate(
            [
                lax.ppermute(tail, axis, [(i, (i + 1) % count) for i in range(ends)]),
                cells,
                lax.ppermute(head, axis, [((i + 1) % count, i) for i in range(ends)]),
            ],
            axis=dim,
        )
    return cells


def shifted(block, axis, distance):
    devices = range(lax.axis_size(axis))
    route = [(i - distance, i) for i in devices if i - distance in devices]
    return lax.ppermute(block, axis, route)


def _lane(x, j, n):
    return jnp.broadcast_to(x[:, j : j + 1], (8, n))


def _diag_kernel(a_ref, li_ref):
    g_count, n, _ = a_ref.shape
    rows = n // 8
    sub = lax.broadcasted_iota(jnp.int32, (8, n), 0)
    lane = lax.broadcasted_iota(jnp.int32, (8, n), 1)
    states = []
    for g in range(g_count):
        left = [a_ref[g, 8 * r : 8 * r + 8, :] for r in range(rows)]
        right = [jnp.where(lane == sub + 8 * r, 1.0, 0.0).astype(jnp.float32) for r in range(rows)]
        scale = [jnp.zeros((8, n), jnp.float32) for r in range(rows)]
        cols = {r: _lane(left[r], 0, n) for r in range(rows)}
        states.append((left, right, scale, cols))
    for j in range(n):
        r0, s = divmod(j, 8)
        for left, right, scale, cols in states:
            row_l = jnp.broadcast_to(left[r0][s : s + 1, :], (8, n))
            row_r = jnp.broadcast_to(right[r0][s : s + 1, :], (8, n))
            piv = jnp.broadcast_to(cols[r0][s : s + 1, :], (8, n))
            inv = 1.0 / piv
            scale[r0] = jnp.where(sub == s, lax.rsqrt(piv), scale[r0])
            if j + 1 < n:
                r1 = (j + 1) // 8
                ahead = {r: _lane(left[r], j + 1, n) for r in range(r1, rows)}
                cross = _lane(row_l, j + 1, n)
                cross = cross * inv
            row_l = row_l * inv
            row_r = row_r * inv
            for r in range(r0, rows):
                new_l = left[r] - cols[r] * row_l
                new_r = right[r] - cols[r] * row_r
                if r == r0:
                    new_l = jnp.where(sub > s, new_l, left[r])
                    new_r = jnp.where(sub > s, new_r, right[r])
                left[r] = new_l
                right[r] = new_r
                if j + 1 < n and r >= r1:
                    cols[r] = ahead[r] - cols[r] * cross
    for g in range(g_count):
        left, right, scale, cols = states[g]
        for r in range(rows):
            li_ref[g, 8 * r : 8 * r + 8, :] = right[r] * scale[r]


def diag_factor(a, points):
    groups, _, _ = a.shape
    block = (groups, points, points)
    return pl.pallas_call(
        _diag_kernel,
        out_shape=jax.ShapeDtypeStruct(block, jnp.float32),
        grid=(1,),
        in_specs=[pl.BlockSpec(block, lambda i: (0, 0, 0))],
        out_specs=pl.BlockSpec(block, lambda i: (0, 0, 0)),
    )(a)


def mm(spec, x, y):
    return jnp.einsum(spec, x, y, precision=lax.Precision.HIGHEST)


def many_blocks(pts, vals, mask):
    groups, slots, _, points = pts.shape
    count = slots * points
    fields = vals.shape[2]
    coords = jnp.transpose(pts, (0, 1, 3, 2)).reshape(groups, count, 2)
    mpts = jnp.repeat(mask, points, axis=1)
    delta_x = coords[:, :, 0][:, :, None] - coords[:, :, 0][:, None, :]
    delta_y = coords[:, :, 1][:, :, None] - coords[:, :, 1][:, None, :]
    scaled = jnp.sqrt(3.0) * jnp.sqrt(delta_x * delta_x + delta_y * delta_y) / ELL
    kernel = (1.0 + scaled) * jnp.exp(-scaled)
    eye = jnp.eye(count, dtype=jnp.float32)
    cov = mpts[:, :, None] * mpts[:, None, :] * kernel + eye * (NUGGET * mpts + 1.0 - mpts)[:, :, None]
    values = jnp.transpose(vals, (0, 1, 3, 2)).reshape(groups, count, fields) * mpts[:, :, None]
    trail = cov
    rest = values
    panels, inverses = [], []
    for k in range(slots):
        inv = diag_factor(trail, points)
        inverses.append(inv)
        white = mm("gij,gjf->gif", inv, rest[:, :points])
        if k < slots - 1:
            panel = mm("gic,gjc->gij", trail[:, points:, :points], inv)
            panels.append(panel)
            trail = trail[:, points:, points:] - mm("gic,gjc->gij", panel, panel)
            rest = rest[:, points:] - mm("gic,gcf->gif", panel, white)
    back = mm("gji,gjf->gif", inverses[-1], white)
    for k in range(slots - 2, -1, -1):
        rhs = -mm("gic,gif->gcf", panels[k], back)
        back = jnp.concatenate([mm("gji,gjf->gif", inverses[k], rhs), back], axis=1)
    back = back * mpts[:, :, None]
    back = jnp.transpose(back.reshape(groups, slots, points, fields), (0, 1, 3, 2))
    return jnp.transpose(white, (0, 2, 1)), back


def fetch_across(local):
    return padded_2(local, (("grp", 1),), 1)


def fetch_older(local):
    older = []
    for distance in (2, 1):
        older.append(shifted(local, "blk", distance))
    return jnp.concatenate(older + [local], axis=0)


def back_across(terms):
    total_count = terms[:, 1:2]
    for column, offset in ((0, -1), (2, 1)):
        total_count = total_count + shifted(terms[:, column : column + 1], "grp", offset)
    return total_count


def back_older(terms):
    per = terms.shape[0] // 3
    farthest = terms[:per]
    nearest = terms[per : 2 * per]
    total_count = terms[2 * per :]
    for distance, piece in ((1, nearest), (2, farthest)):
        total_count = total_count + shifted(piece, "blk", -distance)
    return total_count


def per_device(coords, fields, neighbours):
    per = coords.shape[0]
    window = fetch_older(fetch_across(jnp.concatenate([coords, fields], axis=2)))
    groups = lax.axis_size("grp")
    blk_pos = lax.axis_index("blk")
    grp_pos = lax.axis_index("grp")
    neighbour_lists = neighbours.reshape(per, neighbours.shape[2])
    earlier = neighbour_lists // groups - (blk_pos - 2) * per
    beside = neighbour_lists % groups - grp_pos + 1
    own_slot = ((2 * per + jnp.arange(per, dtype=jnp.int32)) * 3 + 1)[:, None]
    slots = jnp.concatenate(
        [jnp.where(neighbour_lists >= 0, earlier * 3 + beside, own_slot), own_slot], axis=1
    )
    masks = jnp.concatenate(
        [(neighbour_lists >= 0).astype(jnp.float32), jnp.ones((per, 1), jnp.float32)], axis=1
    )
    flat_window = window.reshape((9 * per,) + window.shape[2:])
    width = slots.shape[1]
    local_fields = fields.shape[2]
    points = fields.shape[3]
    rows = flat_window[slots]
    whitened, backs = many_blocks(rows[:, :, :2], rows[:, :, 2:], masks)
    onehot = (slots.reshape(-1)[None, :] == jnp.arange(9 * per, dtype=jnp.int32)[:, None]).astype(
        jnp.float32
    )
    onehot = onehot * masks.reshape(-1)[None, :]
    terms = jnp.dot(
        onehot, backs.reshape(width * per, local_fields * points), precision=lax.Precision.HIGHEST
    )
    terms = terms.reshape(3 * per, 3, local_fields, points)
    product = back_across(back_older(terms))
    return (whitened[:, None], product)


def solution(mesh):
    return jax.shard_map(
        per_device,
        mesh=mesh,
        in_specs=(
            P(("parts", "blk"), "grp", None, None),
            P(("parts", "blk"), "grp", "fld", None),
            P(("parts", "blk"), "grp", None),
        ),
        out_specs=(
            P(("parts", "blk"), "grp", "fld", None),
            P(("parts", "blk"), "grp", "fld", None),
        ),
        check_vma=False,
    )
```

```python
import jax
import jax.numpy as jnp
from jax import lax
from jax.sharding import PartitionSpec as P
from jax.experimental import pallas as pl

ELL = 0.3
NUGGET = 0.25


def padded_2(cells, sides, width):
    for axis, dim in sides:
        count = lax.axis_size(axis)
        ends = count - 1
        head = lax.slice_in_dim(cells, 0, width, axis=dim)
        tail = lax.slice_in_dim(cells, cells.shape[dim] - width, cells.shape[dim], axis=dim)
        cells = jnp.concatenate(
            [
                lax.ppermute(tail, axis, [(i, (i + 1) % count) for i in range(ends)]),
                cells,
                lax.ppermute(head, axis, [((i + 1) % count, i) for i in range(ends)]),
            ],
            axis=dim,
        )
    return cells


def shifted(block, axis, distance):
    devices = range(lax.axis_size(axis))
    route = [(i - distance, i) for i in devices if i - distance in devices]
    return lax.ppermute(block, axis, route)


def _lane(x, j, n):
    return jnp.broadcast_to(x[:, j : j + 1], (8, n))


def _diag_kernel(a_ref, li_ref):
    g_count, n, _ = a_ref.shape
    rows = n // 8
    sub = lax.broadcasted_iota(jnp.int32, (8, n), 0)
    lane = lax.broadcasted_iota(jnp.int32, (8, n), 1)
    states = []
    for g in range(g_count):
        left = [a_ref[g, 8 * r : 8 * r + 8, :] for r in range(rows)]
        right = [jnp.where(lane == sub + 8 * r, 1.0, 0.0).astype(jnp.float32) for r in range(rows)]
        scale = [jnp.zeros((8, n), jnp.float32) for r in range(rows)]
        cols = {r: _lane(left[r], 0, n) for r in range(rows)}
        states.append((left, right, scale, cols))
    for j in range(n):
        r0, s = divmod(j, 8)
        for left, right, scale, cols in states:
            row_l = jnp.broadcast_to(left[r0][s : s + 1, :], (8, n))
            row_r = jnp.broadcast_to(right[r0][s : s + 1, :], (8, n))
            piv = jnp.broadcast_to(cols[r0][s : s + 1, :], (8, n))
            inv = 1.0 / piv
            scale[r0] = jnp.where(sub == s, lax.rsqrt(piv), scale[r0])
            if j + 1 < n:
                r1 = (j + 1) // 8
                ahead = {r: _lane(left[r], j + 1, n) for r in range(r1, rows)}
                s1 = (j + 1) % 8
                cross = jnp.broadcast_to(cols[r1][s1 : s1 + 1, :], (8, n))
                cross = cross * inv
            row_l = row_l * inv
            row_r = row_r * inv
            for r in range(r0, rows):
                new_l = left[r] - cols[r] * row_l
                new_r = right[r] - cols[r] * row_r
                if r == r0:
                    new_l = jnp.where(sub > s, new_l, left[r])
                    new_r = jnp.where(sub > s, new_r, right[r])
                left[r] = new_l
                right[r] = new_r
                if j + 1 < n and r >= r1:
                    cols[r] = ahead[r] - cols[r] * cross
    for g in range(g_count):
        left, right, scale, cols = states[g]
        for r in range(rows):
            li_ref[g, 8 * r : 8 * r + 8, :] = right[r] * scale[r]


def diag_factor(a, points):
    groups, _, _ = a.shape
    block = (groups, points, points)
    return pl.pallas_call(
        _diag_kernel,
        out_shape=jax.ShapeDtypeStruct(block, jnp.float32),
        grid=(1,),
        in_specs=[pl.BlockSpec(block, lambda i: (0, 0, 0))],
        out_specs=pl.BlockSpec(block, lambda i: (0, 0, 0)),
    )(a)


def mm(spec, x, y):
    return jnp.einsum(spec, x, y, precision=lax.Precision.HIGHEST)


def many_blocks(pts, gather_vals, mask, late=2):
    groups, slots, _, points = pts.shape
    count = slots * points
    coords = jnp.transpose(pts, (0, 1, 3, 2)).reshape(groups, count, 2)
    mpts = jnp.repeat(mask, points, axis=1)
    delta_x = coords[:, :, 0][:, :, None] - coords[:, :, 0][:, None, :]
    delta_y = coords[:, :, 1][:, :, None] - coords[:, :, 1][:, None, :]
    scaled = jnp.sqrt(3.0) * jnp.sqrt(delta_x * delta_x + delta_y * delta_y) / ELL
    kernel = (1.0 + scaled) * jnp.exp(-scaled)
    eye = jnp.eye(count, dtype=jnp.float32)
    cov = mpts[:, :, None] * mpts[:, None, :] * kernel + eye * (NUGGET * mpts + 1.0 - mpts)[:, :, None]
    trail = cov
    panels, inverses = [], []
    rest = None
    solved = 0
    for k in range(slots):
        inv = diag_factor(trail, points)
        inverses.append(inv)
        if k == 0:
            vals = gather_vals(inv)
            fields = vals.shape[2]
            values = jnp.transpose(vals, (0, 1, 3, 2)).reshape(groups, count, fields)
            rest = values * mpts[:, :, None]
        if k < slots - 1:
            panel = mm("gic,gjc->gij", trail[:, points:, :points], inv)
            panels.append(panel)
            trail = trail[:, points:, points:] - mm("gic,gjc->gij", panel, panel)
        if k >= min(late, slots - 1):
            while solved <= k:
                white = mm("gij,gjf->gif", inverses[solved], rest[:, :points])
                if solved < slots - 1:
                    rest = rest[:, points:] - mm("gic,gcf->gif", panels[solved], white)
                solved += 1
    back = mm("gji,gjf->gif", inverses[-1], white)
    for k in range(slots - 2, -1, -1):
        rhs = -mm("gic,gif->gcf", panels[k], back)
        back = jnp.concatenate([mm("gji,gjf->gif", inverses[k], rhs), back], axis=1)
    back = back * mpts[:, :, None]
    back = jnp.transpose(back.reshape(groups, slots, points, fields), (0, 1, 3, 2))
    return jnp.transpose(white, (0, 2, 1)), back


def fetch_across(local):
    return padded_2(local, (("grp", 1),), 1)


def fetch_older(local):
    older = []
    for distance in (2, 1):
        older.append(shifted(local, "blk", distance))
    return jnp.concatenate(older + [local], axis=0)


def back_across(terms):
    total_count = terms[:, 1:2]
    for column, offset in ((0, -1), (2, 1)):
        total_count = total_count + shifted(terms[:, column : column + 1], "grp", offset)
    return total_count


def back_older(terms):
    per = terms.shape[0] // 3
    farthest = terms[:per]
    nearest = terms[per : 2 * per]
    total_count = terms[2 * per :]
    for distance, piece in ((1, nearest), (2, farthest)):
        total_count = total_count + shifted(piece, "blk", -distance)
    return total_count


def per_device(coords, fields, neighbours):
    per = coords.shape[0]
    window_coords = fetch_older(fetch_across(coords))
    groups = lax.axis_size("grp")
    blk_pos = lax.axis_index("blk")
    grp_pos = lax.axis_index("grp")
    neighbour_lists = neighbours.reshape(per, neighbours.shape[2])
    earlier = neighbour_lists // groups - (blk_pos - 2) * per
    beside = neighbour_lists % groups - grp_pos + 1
    own_slot = ((2 * per + jnp.arange(per, dtype=jnp.int32)) * 3 + 1)[:, None]
    slots = jnp.concatenate(
        [jnp.where(neighbour_lists >= 0, earlier * 3 + beside, own_slot), own_slot], axis=1
    )
    masks = jnp.concatenate(
        [(neighbour_lists >= 0).astype(jnp.float32), jnp.ones((per, 1), jnp.float32)], axis=1
    )
    flat_coords = window_coords.reshape((9 * per,) + coords.shape[2:])
    width = slots.shape[1]
    local_fields = fields.shape[2]
    points = fields.shape[3]

    def gather_vals(after):
        _, local = lax.optimization_barrier((after, fields))
        window_fields = fetch_older(fetch_across(local))
        flat_fields = window_fields.reshape((9 * per,) + fields.shape[2:])
        return flat_fields[slots]

    whitened, backs = many_blocks(flat_coords[slots], gather_vals, masks)
    onehot = (slots.reshape(-1)[None, :] == jnp.arange(9 * per, dtype=jnp.int32)[:, None]).astype(
        jnp.float32
    )
    onehot = onehot * masks.reshape(-1)[None, :]
    terms = jnp.dot(
        onehot, backs.reshape(width * per, local_fields * points), precision=lax.Precision.HIGHEST
    )
    terms = terms.reshape(3 * per, 3, local_fields, points)
    product = back_across(back_older(terms))
    return (whitened[:, None], product)


def solution(mesh):
    return jax.shard_map(
        per_device,
        mesh=mesh,
        in_specs=(
            P(("parts", "blk"), "grp", None, None),
            P(("parts", "blk"), "grp", "fld", None),
            P(("parts", "blk"), "grp", None),
        ),
        out_specs=(
            P(("parts", "blk"), "grp", "fld", None),
            P(("parts", "blk"), "grp", "fld", None),
        ),
        check_vma=False,
    )
```

```python
import jax
import jax.numpy as jnp
from jax import lax
from jax.sharding import PartitionSpec as P
from jax.experimental import pallas as pl

ELL = 0.3
NUGGET = 0.25


def padded_2(cells, sides, width):
    for axis, dim in sides:
        count = lax.axis_size(axis)
        ends = count - 1
        head = lax.slice_in_dim(cells, 0, width, axis=dim)
        tail = lax.slice_in_dim(cells, cells.shape[dim] - width, cells.shape[dim], axis=dim)
        cells = jnp.concatenate(
            [
                lax.ppermute(tail, axis, [(i, (i + 1) % count) for i in range(ends)]),
                cells,
                lax.ppermute(head, axis, [((i + 1) % count, i) for i in range(ends)]),
            ],
            axis=dim,
        )
    return cells


def shifted(block, axis, distance):
    devices = range(lax.axis_size(axis))
    route = [(i - distance, i) for i in devices if i - distance in devices]
    return lax.ppermute(block, axis, route)


def _lane(x, j, n):
    return jnp.broadcast_to(x[:, j : j + 1], (8, n))


def _diag_kernel(a_ref, li_ref):
    g_count, n, _ = a_ref.shape
    rows = n // 8
    sub = lax.broadcasted_iota(jnp.int32, (8, n), 0)
    lane = lax.broadcasted_iota(jnp.int32, (8, n), 1)
    states = []
    for g in range(g_count):
        left = [a_ref[g, 8 * r : 8 * r + 8, :] for r in range(rows)]
        right = [jnp.where(lane == sub + 8 * r, 1.0, 0.0).astype(jnp.float32) for r in range(rows)]
        scale = [jnp.zeros((8, n), jnp.float32) for r in range(rows)]
        cols = {r: _lane(left[r], 0, n) for r in range(rows)}
        states.append((left, right, scale, cols))
    for j in range(n):
        r0, s = divmod(j, 8)
        for left, right, scale, cols in states:
            row_l = jnp.broadcast_to(left[r0][s : s + 1, :], (8, n))
            row_r = jnp.broadcast_to(right[r0][s : s + 1, :], (8, n))
            piv = jnp.broadcast_to(cols[r0][s : s + 1, :], (8, n))
            root = lax.rsqrt(piv)
            inv = root * root
            scale[r0] = jnp.where(sub == s, root, scale[r0])
            if j + 1 < n:
                r1 = (j + 1) // 8
                ahead = {r: _lane(left[r], j + 1, n) for r in range(r1, rows)}
                s1 = (j + 1) % 8
                cross = jnp.broadcast_to(cols[r1][s1 : s1 + 1, :], (8, n))
                cross = cross * inv
            row_l = row_l * inv
            row_r = row_r * inv
            for r in range(r0, rows):
                new_l = left[r] - cols[r] * row_l
                new_r = right[r] - cols[r] * row_r
                if r == r0:
                    new_l = jnp.where(sub > s, new_l, left[r])
                    new_r = jnp.where(sub > s, new_r, right[r])
                left[r] = new_l
                right[r] = new_r
                if j + 1 < n and r >= r1:
                    cols[r] = ahead[r] - cols[r] * cross
    for g in range(g_count):
        left, right, scale, cols = states[g]
        for r in range(rows):
            li_ref[g, 8 * r : 8 * r + 8, :] = right[r] * scale[r]


def diag_factor(a, points):
    groups, _, _ = a.shape
    block = (groups, points, points)
    return pl.pallas_call(
        _diag_kernel,
        out_shape=jax.ShapeDtypeStruct(block, jnp.float32),
        grid=(1,),
        in_specs=[pl.BlockSpec(block, lambda i: (0, 0, 0))],
        out_specs=pl.BlockSpec(block, lambda i: (0, 0, 0)),
    )(a)


def mm(spec, x, y):
    return jnp.einsum(spec, x, y, precision=lax.Precision.HIGHEST)


def many_blocks(pts, gather_vals, mask, late=2):
    groups, slots, _, points = pts.shape
    count = slots * points
    coords = jnp.transpose(pts, (0, 1, 3, 2)).reshape(groups, count, 2)
    mpts = jnp.repeat(mask, points, axis=1)
    delta_x = coords[:, :, 0][:, :, None] - coords[:, :, 0][:, None, :]
    delta_y = coords[:, :, 1][:, :, None] - coords[:, :, 1][:, None, :]
    scaled = jnp.sqrt(3.0) * jnp.sqrt(delta_x * delta_x + delta_y * delta_y) / ELL
    kernel = (1.0 + scaled) * jnp.exp(-scaled)
    eye = jnp.eye(count, dtype=jnp.float32)
    cov = mpts[:, :, None] * mpts[:, None, :] * kernel + eye * (NUGGET * mpts + 1.0 - mpts)[:, :, None]
    trail = cov
    panels, inverses = [], []
    rest = None
    solved = 0
    for k in range(slots):
        inv = diag_factor(trail, points)
        inverses.append(inv)
        if k == 0:
            vals = gather_vals(inv)
            fields = vals.shape[2]
            values = jnp.transpose(vals, (0, 1, 3, 2)).reshape(groups, count, fields)
            rest = values * mpts[:, :, None]
        if k < slots - 1:
            panel = mm("gic,gjc->gij", trail[:, points:, :points], inv)
            panels.append(panel)
            trail = trail[:, points:, points:] - mm("gic,gjc->gij", panel, panel)
        if k >= min(late, slots - 1):
            while solved <= k:
                white = mm("gij,gjf->gif", inverses[solved], rest[:, :points])
                if solved < slots - 1:
                    rest = rest[:, points:] - mm("gic,gcf->gif", panels[solved], white)
                solved += 1
    back = mm("gji,gjf->gif", inverses[-1], white)
    for k in range(slots - 2, -1, -1):
        rhs = -mm("gic,gif->gcf", panels[k], back)
        back = jnp.concatenate([mm("gji,gjf->gif", inverses[k], rhs), back], axis=1)
    back = back * mpts[:, :, None]
    back = jnp.transpose(back.reshape(groups, slots, points, fields), (0, 1, 3, 2))
    return jnp.transpose(white, (0, 2, 1)), back


def fetch_across(local):
    return padded_2(local, (("grp", 1),), 1)


def fetch_older(local):
    older = []
    for distance in (2, 1):
        older.append(shifted(local, "blk", distance))
    return jnp.concatenate(older + [local], axis=0)


def back_across(terms):
    total_count = terms[:, 1:2]
    for column, offset in ((0, -1), (2, 1)):
        total_count = total_count + shifted(terms[:, column : column + 1], "grp", offset)
    return total_count


def back_older(terms):
    per = terms.shape[0] // 3
    farthest = terms[:per]
    nearest = terms[per : 2 * per]
    total_count = terms[2 * per :]
    for distance, piece in ((1, nearest), (2, farthest)):
        total_count = total_count + shifted(piece, "blk", -distance)
    return total_count


def per_device(coords, fields, neighbours):
    per = coords.shape[0]
    window_coords = fetch_older(fetch_across(coords))
    groups = lax.axis_size("grp")
    blk_pos = lax.axis_index("blk")
    grp_pos = lax.axis_index("grp")
    neighbour_lists = neighbours.reshape(per, neighbours.shape[2])
    earlier = neighbour_lists // groups - (blk_pos - 2) * per
    beside = neighbour_lists % groups - grp_pos + 1
    own_slot = ((2 * per + jnp.arange(per, dtype=jnp.int32)) * 3 + 1)[:, None]
    slots = jnp.concatenate(
        [jnp.where(neighbour_lists >= 0, earlier * 3 + beside, own_slot), own_slot], axis=1
    )
    masks = jnp.concatenate(
        [(neighbour_lists >= 0).astype(jnp.float32), jnp.ones((per, 1), jnp.float32)], axis=1
    )
    flat_coords = window_coords.reshape((9 * per,) + coords.shape[2:])
    width = slots.shape[1]
    local_fields = fields.shape[2]
    points = fields.shape[3]

    def gather_vals(after):
        _, local = lax.optimization_barrier((after, fields))
        window_fields = fetch_older(fetch_across(local))
        flat_fields = window_fields.reshape((9 * per,) + fields.shape[2:])
        return flat_fields[slots]

    whitened, backs = many_blocks(flat_coords[slots], gather_vals, masks)
    onehot = (slots.reshape(-1)[None, :] == jnp.arange(9 * per, dtype=jnp.int32)[:, None]).astype(
        jnp.float32
    )
    onehot = onehot * masks.reshape(-1)[None, :]
    terms = jnp.dot(
        onehot, backs.reshape(width * per, local_fields * points), precision=lax.Precision.HIGHEST
    )
    terms = terms.reshape(3 * per, 3, local_fields, points)
    product = back_across(back_older(terms))
    return (whitened[:, None], product)


def solution(mesh):
    return jax.shard_map(
        per_device,
        mesh=mesh,
        in_specs=(
            P(("parts", "blk"), "grp", None, None),
            P(("parts", "blk"), "grp", "fld", None),
            P(("parts", "blk"), "grp", None),
        ),
        out_specs=(
            P(("parts", "blk"), "grp", "fld", None),
            P(("parts", "blk"), "grp", "fld", None),
        ),
        check_vma=False,
    )
```

```python
import jax
import jax.numpy as jnp
from jax import lax
from jax.sharding import PartitionSpec as P
from jax.experimental import pallas as pl

ELL = 0.3
NUGGET = 0.25


def padded_2(cells, sides, width):
    for axis, dim in sides:
        count = lax.axis_size(axis)
        ends = count - 1
        head = lax.slice_in_dim(cells, 0, width, axis=dim)
        tail = lax.slice_in_dim(cells, cells.shape[dim] - width, cells.shape[dim], axis=dim)
        cells = jnp.concatenate(
            [
                lax.ppermute(tail, axis, [(i, (i + 1) % count) for i in range(ends)]),
                cells,
                lax.ppermute(head, axis, [((i + 1) % count, i) for i in range(ends)]),
            ],
            axis=dim,
        )
    return cells


def shifted(block, axis, distance):
    devices = range(lax.axis_size(axis))
    route = [(i - distance, i) for i in devices if i - distance in devices]
    return lax.ppermute(block, axis, route)


def _lane(x, j, n):
    return jnp.broadcast_to(x[:, j : j + 1], (8, n))


def _diag_kernel(a_ref, li_ref):
    g_count, n, _ = a_ref.shape
    rows = n // 8
    sub = lax.broadcasted_iota(jnp.int32, (8, n), 0)
    lane = lax.broadcasted_iota(jnp.int32, (8, n), 1)
    states = []
    for g in range(g_count):
        left = [a_ref[g, 8 * r : 8 * r + 8, :] for r in range(rows)]
        right = [jnp.where(lane == sub + 8 * r, 1.0, 0.0).astype(jnp.float32) for r in range(rows)]
        scale = [jnp.zeros((8, n), jnp.float32) for r in range(rows)]
        cols = {r: _lane(left[r], 0, n) for r in range(rows)}
        states.append((left, right, scale, cols))
    for j in range(n):
        r0, s = divmod(j, 8)
        for left, right, scale, cols in states:
            row_l = jnp.broadcast_to(left[r0][s : s + 1, :], (8, n))
            row_r = jnp.broadcast_to(right[r0][s : s + 1, :], (8, n))
            piv = jnp.broadcast_to(cols[r0][s : s + 1, :], (8, n))
            root = lax.rsqrt(piv)
            inv = root * root
            scale[r0] = jnp.where(sub == s, root, scale[r0])
            if j + 1 < n:
                r1 = (j + 1) // 8
                ahead = {r: _lane(left[r], j + 1, n) for r in range(r1, rows)}
                s1 = (j + 1) % 8
                cross = jnp.broadcast_to(cols[r1][s1 : s1 + 1, :], (8, n))
                cross = cross * inv
            row_l = row_l * inv
            row_r = row_r * inv
            for r in range(r0, rows):
                new_l = left[r] - cols[r] * row_l
                new_r = right[r] - cols[r] * row_r
                if r == r0:
                    new_r = jnp.where(sub > s, new_r, right[r])
                left[r] = new_l
                right[r] = new_r
                if j + 1 < n and r >= r1:
                    cols[r] = ahead[r] - cols[r] * cross
    for g in range(g_count):
        left, right, scale, cols = states[g]
        for r in range(rows):
            li_ref[g, 8 * r : 8 * r + 8, :] = right[r] * scale[r]


def diag_factor(a, points):
    groups, _, _ = a.shape
    block = (groups, points, points)
    return pl.pallas_call(
        _diag_kernel,
        out_shape=jax.ShapeDtypeStruct(block, jnp.float32),
        grid=(1,),
        in_specs=[pl.BlockSpec(block, lambda i: (0, 0, 0))],
        out_specs=pl.BlockSpec(block, lambda i: (0, 0, 0)),
    )(a)


def mm(spec, x, y):
    return jnp.einsum(spec, x, y, precision=lax.Precision.HIGHEST)


def many_blocks(pts, gather_vals, mask, late=2):
    groups, slots, _, points = pts.shape
    count = slots * points
    coords = jnp.transpose(pts, (0, 1, 3, 2)).reshape(groups, count, 2)
    mpts = jnp.repeat(mask, points, axis=1)
    delta_x = coords[:, :, 0][:, :, None] - coords[:, :, 0][:, None, :]
    delta_y = coords[:, :, 1][:, :, None] - coords[:, :, 1][:, None, :]
    scaled = jnp.sqrt(3.0) * jnp.sqrt(delta_x * delta_x + delta_y * delta_y) / ELL
    kernel = (1.0 + scaled) * jnp.exp(-scaled)
    eye = jnp.eye(count, dtype=jnp.float32)
    cov = mpts[:, :, None] * mpts[:, None, :] * kernel + eye * (NUGGET * mpts + 1.0 - mpts)[:, :, None]
    trail = cov
    panels, inverses = [], []
    rest = None
    solved = 0
    for k in range(slots):
        inv = diag_factor(trail, points)
        inverses.append(inv)
        if k == 0:
            vals = gather_vals(inv)
            fields = vals.shape[2]
            values = jnp.transpose(vals, (0, 1, 3, 2)).reshape(groups, count, fields)
            rest = values * mpts[:, :, None]
        if k < slots - 1:
            panel = mm("gic,gjc->gij", trail[:, points:, :points], inv)
            panels.append(panel)
            trail = trail[:, points:, points:] - mm("gic,gjc->gij", panel, panel)
        if k >= min(late, slots - 1):
            while solved <= k:
                white = mm("gij,gjf->gif", inverses[solved], rest[:, :points])
                if solved < slots - 1:
                    rest = rest[:, points:] - mm("gic,gcf->gif", panels[solved], white)
                solved += 1
    back = mm("gji,gjf->gif", inverses[-1], white)
    for k in range(slots - 2, -1, -1):
        rhs = -mm("gic,gif->gcf", panels[k], back)
        back = jnp.concatenate([mm("gji,gjf->gif", inverses[k], rhs), back], axis=1)
    back = back * mpts[:, :, None]
    back = jnp.transpose(back.reshape(groups, slots, points, fields), (0, 1, 3, 2))
    return jnp.transpose(white, (0, 2, 1)), back


def fetch_across(local):
    return padded_2(local, (("grp", 1),), 1)


def fetch_older(local):
    older = []
    for distance in (2, 1):
        older.append(shifted(local, "blk", distance))
    return jnp.concatenate(older + [local], axis=0)


def back_across(terms):
    total_count = terms[:, 1:2]
    for column, offset in ((0, -1), (2, 1)):
        total_count = total_count + shifted(terms[:, column : column + 1], "grp", offset)
    return total_count


def back_older(terms):
    per = terms.shape[0] // 3
    farthest = terms[:per]
    nearest = terms[per : 2 * per]
    total_count = terms[2 * per :]
    for distance, piece in ((1, nearest), (2, farthest)):
        total_count = total_count + shifted(piece, "blk", -distance)
    return total_count


def per_device(coords, fields, neighbours):
    per = coords.shape[0]
    window_coords = fetch_older(fetch_across(coords))
    groups = lax.axis_size("grp")
    blk_pos = lax.axis_index("blk")
    grp_pos = lax.axis_index("grp")
    neighbour_lists = neighbours.reshape(per, neighbours.shape[2])
    earlier = neighbour_lists // groups - (blk_pos - 2) * per
    beside = neighbour_lists % groups - grp_pos + 1
    own_slot = ((2 * per + jnp.arange(per, dtype=jnp.int32)) * 3 + 1)[:, None]
    slots = jnp.concatenate(
        [jnp.where(neighbour_lists >= 0, earlier * 3 + beside, own_slot), own_slot], axis=1
    )
    masks = jnp.concatenate(
        [(neighbour_lists >= 0).astype(jnp.float32), jnp.ones((per, 1), jnp.float32)], axis=1
    )
    flat_coords = window_coords.reshape((9 * per,) + coords.shape[2:])
    width = slots.shape[1]
    local_fields = fields.shape[2]
    points = fields.shape[3]

    def gather_vals(after):
        _, local = lax.optimization_barrier((after, fields))
        window_fields = fetch_older(fetch_across(local))
        flat_fields = window_fields.reshape((9 * per,) + fields.shape[2:])
        return flat_fields[slots]

    whitened, backs = many_blocks(flat_coords[slots], gather_vals, masks)
    onehot = (slots.reshape(-1)[None, :] == jnp.arange(9 * per, dtype=jnp.int32)[:, None]).astype(
        jnp.float32
    )
    onehot = onehot * masks.reshape(-1)[None, :]
    terms = jnp.dot(
        onehot, backs.reshape(width * per, local_fields * points), precision=lax.Precision.HIGHEST
    )
    terms = terms.reshape(3 * per, 3, local_fields, points)
    product = back_across(back_older(terms))
    return (whitened[:, None], product)


def solution(mesh):
    return jax.shard_map(
        per_device,
        mesh=mesh,
        in_specs=(
            P(("parts", "blk"), "grp", None, None),
            P(("parts", "blk"), "grp", "fld", None),
            P(("parts", "blk"), "grp", None),
        ),
        out_specs=(
            P(("parts", "blk"), "grp", "fld", None),
            P(("parts", "blk"), "grp", "fld", None),
        ),
        check_vma=False,
    )
```
